256 devices in a mesh: dp: 8 (over z_hi, x), ctx: 32 (over y, z_lo, core).
Axes of the slice: x: 4, y: 4, z: 8 (z_hi: 2, z_lo: 4; z = z_hi * 4 + z_lo), core: 2. Of those that a mesh axis runs over, the one named last changes fastest.
Arguments:
- y_first: bfloat16 [8, 4096, 1024], P('dp', 'ctx'), may hold values from -6 to 6
- x_second: bfloat16 [8, 4096, 1024], P('dp', 'ctx'), may hold values from -40 to 40
- grad_first: bfloat16 [8, 4096, 1024], P('dp', 'ctx'), may hold values from -6 to 6
- grad_second: bfloat16 [8, 4096, 1024], P('dp', 'ctx'), may hold values from -6 to 6
- w_query: bfloat16 [1024, 1024], P('dp'), may hold values from -0.1875 to 0.1875
- w_key: bfloat16 [1024, 1024], P('dp'), may hold values from -0.1875 to 0.1875
- w_value: bfloat16 [1024, 1024], P('dp'), may hold values from -0.1875 to 0.1875
- w_out: bfloat16 [1024, 1024], P('dp'), may hold values from -0.1875 to 0.1875
Outputs:
- x_first: bfloat16 [8, 4096, 1024], P('dp', 'ctx')
- grad_x_second: bfloat16 [8, 4096, 1024], P('dp', 'ctx')
- grad_query: float32 [1024, 1024], P(('dp', 'ctx'))
- grad_out: float32 [1024, 1024], P(('dp', 'ctx'))
The draws below stay inside these ranges and needn't reach their ends.
All inputs are finite; a program needn't handle non-finite values.
Results may differ from the reference program's by a relative error of at most 0.012.
The reference program's roundings to bfloat16 on the way count: a program that leaves them out, or rounds other values in their place, can miss the bound.
Values may be sent and summed in bfloat16 or wider, within the bound.
No kernel may reach another device: no remote copies, remote signals or barrier semaphores. Data moves between devices by JAX's collectives and lax.ppermute only.
A program may use at most 128 MiB of HBM per device.

```python
import jax
import jax.numpy as jnp
from jax import lax

D = 1024
HEADS = 8
HEAD_DIM = 128
TOK_DEV = 128
SEQS = 8
LENGTH = 4096
TOKENS = 32768
N_CTX = 32


def draw_x_second(key, part):
    key_base, key_rows, key_cols = jax.random.split(jax.random.fold_in(key, 17), 3)
    shape = (SEQS, LENGTH, D)
    row_scale = jnp.exp(jax.random.uniform(key_rows, (SEQS, LENGTH, 1), jnp.float32, -1.15, 1.15))
    col_scale = jnp.exp(jax.random.uniform(key_cols, (1, 1, D), jnp.float32, -1.15, 1.15))
    base = jnp.clip(jax.random.normal(key_base, shape, jnp.float32), -4.0, 4.0)
    return (base * row_scale * col_scale).astype(jnp.bfloat16)


def block_scale(stream_key, shape, cuts, smallest, high):
    def one(position, blocks):
        heights = jax.random.uniform(jax.random.fold_in(jax.random.fold_in(stream_key, 6), position), (blocks,), jnp.float32, smallest / len(cuts), high / len(cuts))
        return jnp.repeat(jnp.exp(heights), shape[position] // blocks).reshape((-1,) + (1,) * (len(shape) - position - 1))

    level = one(*cuts[0])
    for cut in cuts[1:]:
        level = level * one(*cut)
    return level


def scatter_about(key, extent, width, reach, cuts=(), kind=jnp.bfloat16):
    factor_of = block_scale(key, extent, cuts, -0.22, 0.18) if cuts else 1.0
    entries = jax.random.normal(key, extent, jnp.float32) * width * factor_of
    return jnp.minimum(jnp.maximum(entries, -reach), reach).astype(kind)


def setup_inputs(seed: int = 0) -> dict:
    key_list = jax.random.split(jax.random.key(seed), 9)
    return {
        "y_first": scatter_about(key_list[0], (SEQS, LENGTH, D), 1.0, 6.0, ((0, 8), (1, 32))),
        "x_second": draw_x_second(jax.random.fold_in(key_list[8], 71), 0),
        "grad_first": scatter_about(key_list[2], (SEQS, LENGTH, D), 1.0, 6.0, ((0, 8), (1, 32))),
        "grad_second": scatter_about(key_list[3], (SEQS, LENGTH, D), 1.0, 6.0, ((0, 8), (1, 32))),
        "w_query": scatter_about(key_list[4], (D, D), D ** -0.5, 0.1875, ((0, 8),)),
        "w_key": scatter_about(key_list[5], (D, D), D ** -0.5, 0.1875, ((0, 8),)),
        "w_value": scatter_about(key_list[6], (D, D), D ** -0.5, 0.1875, ((0, 8),)),
        "w_out": scatter_about(key_list[7], (D, D), D ** -0.5, 0.1875, ((0, 8),)),
    }


def rounded(value):
    return lax.optimization_barrier(value.astype(jnp.bfloat16)).astype(jnp.float32)

def reference(y_first, x_second, grad_first, grad_second, w_query, w_key, w_value, w_out):
    wide_type = jnp.float32
    causal = jnp.tril(jnp.ones((TOK_DEV, TOK_DEV), dtype=bool))

    def one_sequence(items):
        first_y, second_x, first_grad, second_grad = items
        second_wide = second_x.astype(wide_type)
        inv_rms = lax.rsqrt(lax.optimization_barrier(jnp.mean(second_wide * second_wide, -1, keepdims=True)) + 1e-06)
        normed_wide = second_wide * inv_rms
        normed = normed_wide.astype(jnp.bfloat16)

        def project(weight):
            made = jnp.dot(normed, weight, preferred_element_type=jnp.float32).astype(jnp.bfloat16)
            return made.reshape(N_CTX, TOK_DEV, HEADS, HEAD_DIM)
        queries = project(w_query)
        keys_all = project(w_key)
        values = project(w_value)
        query_wide = queries.astype(wide_type)
        key_wide = keys_all.astype(wide_type)
        value_wide = values.astype(wide_type)
        local_state = jnp.einsum('nthe,nthf->nhef', key_wide, value_wide)
        before = rounded(jnp.cumsum(local_state, 0) - local_state)
        scores = jnp.einsum('nthe,nshe->nhts', query_wide, key_wide)
        scores = rounded(jnp.where(causal[None, None], scores, 0.0))
        mixed = jnp.einsum('nhts,nshf->nthf', scores, value_wide) + jnp.einsum('nthe,nhef->nthf', query_wide, before)
        inv_head = lax.rsqrt(lax.optimization_barrier(jnp.mean(mixed * mixed, -1, keepdims=True)) + 1e-06)
        unit = mixed * inv_head
        attn_out = unit.astype(jnp.bfloat16).reshape(LENGTH, D)
        attended = jnp.dot(attn_out, w_out, preferred_element_type=jnp.float32)
        first_x = (first_y.astype(wide_type) - attended).astype(jnp.bfloat16)
        grad_unit = jnp.dot(first_grad, w_out.T, preferred_element_type=jnp.float32)
        grad_unit = grad_unit.reshape(N_CTX, TOK_DEV, HEADS, HEAD_DIM)
        grad_mixed = inv_head * (grad_unit - unit * lax.optimization_barrier(jnp.mean(grad_unit * unit, -1, keepdims=True)))
        grad_mixed = rounded(grad_mixed)
        score_grad = jnp.einsum('nthf,nshf->nhts', grad_mixed, value_wide)
        score_grad = rounded(jnp.where(causal[None, None], score_grad, 0.0))
        grad_local = jnp.einsum('nthe,nthf->nhef', query_wide, grad_mixed)
        after_state = rounded(jnp.cumsum(grad_local[::-1], 0)[::-1] - grad_local)
        query_grad = jnp.einsum('nhts,nshe->nthe', score_grad, key_wide) + jnp.einsum('nthf,nhef->nthe', grad_mixed, before)
        key_grad = jnp.einsum('nhts,nthe->nshe', score_grad, query_wide) + jnp.einsum('nshf,nhef->nshe', value_wide, after_state)
        value_grad = jnp.einsum('nhts,nthf->nshf', scores, grad_mixed) + jnp.einsum('nshe,nhef->nshf', key_wide, after_state)
        query_grad = query_grad.astype(jnp.bfloat16).reshape(LENGTH, D)
        key_grad = key_grad.astype(jnp.bfloat16).reshape(LENGTH, D)
        value_grad = value_grad.astype(jnp.bfloat16).reshape(LENGTH, D)
        grad_normed = jnp.dot(query_grad, w_query.T, preferred_element_type=jnp.float32)
        grad_normed = grad_normed + jnp.dot(key_grad, w_key.T, preferred_element_type=jnp.float32)
        grad_normed = grad_normed + jnp.dot(value_grad, w_value.T, preferred_element_type=jnp.float32)
        back = inv_rms * (grad_normed - normed_wide * lax.optimization_barrier(jnp.mean(grad_normed * normed_wide, -1, keepdims=True)))
        second_out = (second_grad.astype(wide_type) + back).astype(jnp.bfloat16)
        return (first_x, second_out, normed, attn_out, query_grad)
    results = lax.map(one_sequence, (y_first, x_second, grad_first, grad_second))
    first_x, second_out, normed, attn_out, query_grad = results
    factor = float(TOKENS) ** (-0.5)

    def weight_grad(left, right):
        return factor * jnp.dot(left.reshape(-1, D).T, right.reshape(-1, D), preferred_element_type=jnp.float32)
    return (first_x, second_out, weight_grad(normed, query_grad), weight_grad(attn_out, grad_first))
```

```python
import jax
import jax.numpy as jnp
from jax import lax
from jax.sharding import PartitionSpec as P

HEADS = 8
HEAD_DIM = 128


def scan_sum(shard, axis, reverse):
    count = lax.axis_size(axis)
    total = shard
    step = 1
    while step < count:
        if reverse:
            pairs = [(source, source - step) for source in range(step, count)]
        else:
            pairs = [(source, source + step) for source in range(count - step)]
        total = total + lax.ppermute(total, axis, pairs)
        step *= 2
    return total


def gather_rows(weights, piece):
    place = lax.axis_index("ctx")
    parts = [lax.dynamic_slice_in_dim(weight, place * piece, piece, 0) for weight in weights]
    joined = jnp.concatenate(parts, 0)
    gathered = lax.all_gather(joined, ("dp", "ctx"), axis=0, tiled=True)
    gathered = gathered.reshape(-1, len(weights), piece, joined.shape[1])
    return tuple(
        gathered[:, index].reshape(-1, joined.shape[1]) for index in range(len(weights))
    )


def weight_grads(pairs, factor, owners):
    width = pairs[0][0].shape[1]
    blocks = []
    for left, right in pairs:
        made = lax.dot_general(
            left, right, (((0,), (0,)), ((), ())), preferred_element_type=jnp.float32
        )
        blocks.append((factor * made).reshape(owners, -1, width))
    rows = blocks[0].shape[1]
    stacked = jnp.concatenate(blocks, 1).reshape(-1, width)
    share = lax.psum_scatter(stacked, ("dp", "ctx"), scatter_dimension=0, tiled=True)
    return tuple(share[index * rows : (index + 1) * rows] for index in range(len(pairs)))


def on_device(y_first, x_second, grad_first, grad_second, w_query, w_key, w_value, w_out):
    batch, tokens_here, width = y_first.shape
    owners = lax.axis_size("dp") * lax.axis_size("ctx")
    factor = float(batch * tokens_here * owners) ** (-0.5)
    piece = w_query.shape[0] // lax.axis_size("ctx")
    full_query, full_key, full_value = gather_rows((w_query, w_key, w_value), piece)
    (full_out,) = gather_rows((w_out,), piece)
    second_wide = x_second.astype(jnp.float32)
    inv_rms = lax.rsqrt(jnp.mean(second_wide * second_wide, -1, keepdims=True) + 1e-06)
    normed_wide = second_wide * inv_rms
    normed = normed_wide.astype(jnp.bfloat16)

    def project(weight):
        made = jnp.einsum("btd,df->btf", normed, weight, preferred_element_type=jnp.float32)
        return made.astype(jnp.bfloat16).reshape(batch, tokens_here, HEADS, HEAD_DIM)

    queries = project(full_query)
    key_rows = project(full_key)
    values = project(full_value)
    local_state = jnp.einsum(
        "bthe,bthf->bhef", key_rows, values, preferred_element_type=jnp.float32
    )
    before = (scan_sum(local_state, "ctx", False) - local_state).astype(jnp.bfloat16)
    causal = jnp.tril(jnp.ones((tokens_here, tokens_here), dtype=bool))
    scores = jnp.einsum("bthe,bshe->bhts", queries, key_rows, preferred_element_type=jnp.float32)
    scores = jnp.where(causal[None, None], scores, 0.0).astype(jnp.bfloat16)
    mixed = jnp.einsum("bhts,bshf->bthf", scores, values, preferred_element_type=jnp.float32)
    mixed = mixed + jnp.einsum(
        "bthe,bhef->bthf", queries, before, preferred_element_type=jnp.float32
    )
    inv_head = lax.rsqrt(jnp.mean(mixed * mixed, -1, keepdims=True) + 1e-06)
    unit = mixed * inv_head
    attn_out = unit.astype(jnp.bfloat16).reshape(batch, tokens_here, width)
    attended = jnp.einsum("btf,fd->btd", attn_out, full_out, preferred_element_type=jnp.float32)
    x_first = (y_first.astype(jnp.float32) - attended).astype(jnp.bfloat16)
    grad_unit = jnp.einsum("btd,fd->btf", grad_first, full_out, preferred_element_type=jnp.float32)
    grad_unit = grad_unit.reshape(batch, tokens_here, HEADS, HEAD_DIM)
    grad_mixed = inv_head * (grad_unit - unit * jnp.mean(grad_unit * unit, -1, keepdims=True))
    grad_mixed = grad_mixed.astype(jnp.bfloat16)
    score_grad = jnp.einsum(
        "bthf,bshf->bhts", grad_mixed, values, preferred_element_type=jnp.float32
    )
    score_grad = jnp.where(causal[None, None], score_grad, 0.0).astype(jnp.bfloat16)
    grad_local = jnp.einsum(
        "bthe,bthf->bhef", queries, grad_mixed, preferred_element_type=jnp.float32
    )
    after_state = (scan_sum(grad_local, "ctx", True) - grad_local).astype(jnp.bfloat16)
    query_grad = jnp.einsum(
        "bhts,bshe->bthe", score_grad, key_rows, preferred_element_type=jnp.float32
    )
    query_grad = query_grad + jnp.einsum(
        "bthf,bhef->bthe", grad_mixed, before, preferred_element_type=jnp.float32
    )
    key_grad = jnp.einsum(
        "bhts,bthe->bshe", score_grad, queries, preferred_element_type=jnp.float32
    )
    key_grad = key_grad + jnp.einsum(
        "bshf,bhef->bshe", values, after_state, preferred_element_type=jnp.float32
    )
    value_grad = jnp.einsum(
        "bhts,bthf->bshf", scores, grad_mixed, preferred_element_type=jnp.float32
    )
    value_grad = value_grad + jnp.einsum(
        "bshe,bhef->bshf", key_rows, after_state, preferred_element_type=jnp.float32
    )
    query_grad = query_grad.astype(jnp.bfloat16).reshape(batch, tokens_here, width)
    key_grad = key_grad.astype(jnp.bfloat16).reshape(batch, tokens_here, width)
    value_grad = value_grad.astype(jnp.bfloat16).reshape(batch, tokens_here, width)
    grad_normed = jnp.einsum(
        "btf,df->btd", query_grad, full_query, preferred_element_type=jnp.float32
    )
    grad_normed = grad_normed + jnp.einsum(
        "btf,df->btd", key_grad, full_key, preferred_element_type=jnp.float32
    )
    grad_normed = grad_normed + jnp.einsum(
        "btf,df->btd", value_grad, full_value, preferred_element_type=jnp.float32
    )
    back = inv_rms * (
        grad_normed - normed_wide * jnp.mean(grad_normed * normed_wide, -1, keepdims=True)
    )
    grad_x_second = (grad_second.astype(jnp.float32) + back).astype(jnp.bfloat16)
    pairs = (
        (normed.reshape(-1, width), query_grad.reshape(-1, width)),
        (attn_out.reshape(-1, width), grad_first.reshape(-1, width)),
    )
    grad_query, grad_out = weight_grads(pairs, factor, owners)
    return (x_first, grad_x_second, grad_query, grad_out)


def solution(mesh):
    placed = (
        P("dp", "ctx", None),
        P("dp", "ctx", None),
        P("dp", "ctx", None),
        P("dp", "ctx", None),
        P("dp", None),
        P("dp", None),
        P("dp", None),
        P("dp", None),
    )
    return jax.shard_map(
        on_device,
        mesh=mesh,
        in_specs=placed,
        out_specs=(
            P("dp", "ctx", None),
            P("dp", "ctx", None),
            P(("dp", "ctx"), None),
            P(("dp", "ctx"), None),
        ),
        check_vma=False,
    )
```

```python
import jax
import jax.numpy as jnp
from jax import lax
from jax.sharding import PartitionSpec as P

HEADS = 8
HEAD_DIM = 128


def scan_sum(shard, axis, reverse):
    count = lax.axis_size(axis)
    total = shard
    step = 1
    while step < count:
        if reverse:
            pairs = [(source, source - step) for source in range(step, count)]
        else:
            pairs = [(source, source + step) for source in range(count - step)]
        total = total + lax.ppermute(total, axis, pairs)
        step *= 2
    return total


def gather_rows(weights, piece):
    place = lax.axis_index("ctx")
    width = weights[0].shape[1]
    parts = [lax.dynamic_slice_in_dim(weight, place * piece, piece, 0) for weight in weights]
    joined = jnp.concatenate(parts, 0)
    across = lax.all_gather(joined, "dp", axis=0, tiled=False)
    return across.reshape(across.shape[0], len(weights), piece, width)


def spread_rows(across):
    blocks, count, piece, width = across.shape
    gathered = lax.all_gather(across, "ctx", axis=0, tiled=False)
    gathered = jnp.transpose(gathered, (2, 1, 0, 3, 4))
    return tuple(
        gathered[index].reshape(-1, width) for index in range(count)
    )


def weight_grads(pairs, factor):
    width = pairs[0][0].shape[1]
    outer, inner = lax.axis_size("dp"), lax.axis_size("ctx")
    blocks = []
    for left, right in pairs:
        made = lax.dot_general(
            left, right, (((0,), (0,)), ((), ())), preferred_element_type=jnp.float32
        )
        blocks.append((factor * made).reshape(outer, inner, -1, width))
    rows = blocks[0].shape[2]
    stacked = jnp.concatenate(blocks, 2)
    stacked = jnp.transpose(stacked, (1, 0, 2, 3)).reshape(-1, width)
    share = lax.psum_scatter(stacked, "ctx", scatter_dimension=0, tiled=True)
    share = lax.psum_scatter(share, "dp", scatter_dimension=0, tiled=True)
    return tuple(share[index * rows : (index + 1) * rows] for index in range(len(pairs)))


def on_device(y_first, x_second, grad_first, grad_second, w_query, w_key, w_value, w_out):
    batch, tokens_here, width = y_first.shape
    owners = lax.axis_size("dp") * lax.axis_size("ctx")
    factor = float(batch * tokens_here * owners) ** (-0.5)
    piece = w_query.shape[0] // lax.axis_size("ctx")
    across = gather_rows((w_query, w_key, w_value, w_out), piece)
    full_query, full_key, full_value = spread_rows(across[:, :3])
    (full_out,) = spread_rows(across[:, 3:])
    second_wide = x_second.astype(jnp.float32)
    inv_rms = lax.rsqrt(jnp.mean(second_wide * second_wide, -1, keepdims=True) + 1e-06)
    normed_wide = second_wide * inv_rms
    normed = normed_wide.astype(jnp.bfloat16)

    def project(weight):
        made = jnp.einsum("btd,df->btf", normed, weight, preferred_element_type=jnp.float32)
        return made.astype(jnp.bfloat16).reshape(batch, tokens_here, HEADS, HEAD_DIM)

    queries = project(full_query)
    key_rows = project(full_key)
    values = project(full_value)
    local_state = jnp.einsum(
        "bthe,bthf->bhef", key_rows, values, preferred_element_type=jnp.float32
    )
    before = (scan_sum(local_state, "ctx", False) - local_state).astype(jnp.bfloat16)
    causal = jnp.tril(jnp.ones((tokens_here, tokens_here), dtype=bool))
    scores = jnp.einsum("bthe,bshe->bhts", queries, key_rows, preferred_element_type=jnp.float32)
    scores = jnp.where(causal[None, None], scores, 0.0).astype(jnp.bfloat16)
    mixed = jnp.einsum("bhts,bshf->bthf", scores, values, preferred_element_type=jnp.float32)
    mixed = mixed + jnp.einsum(
        "bthe,bhef->bthf", queries, before, preferred_element_type=jnp.float32
    )
    inv_head = lax.rsqrt(jnp.mean(mixed * mixed, -1, keepdims=True) + 1e-06)
    unit = mixed * inv_head
    attn_out = unit.astype(jnp.bfloat16).reshape(batch, tokens_here, width)
    attended = jnp.einsum("btf,fd->btd", attn_out, full_out, preferred_element_type=jnp.float32)
    x_first = (y_first.astype(jnp.float32) - attended).astype(jnp.bfloat16)
    grad_unit = jnp.einsum("btd,fd->btf", grad_first, full_out, preferred_element_type=jnp.float32)
    grad_unit = grad_unit.reshape(batch, tokens_here, HEADS, HEAD_DIM)
    grad_mixed = inv_head * (grad_unit - unit * jnp.mean(grad_unit * unit, -1, keepdims=True))
    grad_mixed = grad_mixed.astype(jnp.bfloat16)
    score_grad = jnp.einsum(
        "bthf,bshf->bhts", grad_mixed, values, preferred_element_type=jnp.float32
    )
    score_grad = jnp.where(causal[None, None], score_grad, 0.0).astype(jnp.bfloat16)
    grad_local = jnp.einsum(
        "bthe,bthf->bhef", queries, grad_mixed, preferred_element_type=jnp.float32
    )
    after_state = (scan_sum(grad_local, "ctx", True) - grad_local).astype(jnp.bfloat16)
    query_grad = jnp.einsum(
        "bhts,bshe->bthe", score_grad, key_rows, preferred_element_type=jnp.float32
    )
    query_grad = query_grad + jnp.einsum(
        "bthf,bhef->bthe", grad_mixed, before, preferred_element_type=jnp.float32
    )
    key_grad = jnp.einsum(
        "bhts,bthe->bshe", score_grad, queries, preferred_element_type=jnp.float32
    )
    key_grad = key_grad + jnp.einsum(
        "bshf,bhef->bshe", values, after_state, preferred_element_type=jnp.float32
    )
    value_grad = jnp.einsum(
        "bhts,bthf->bshf", scores, grad_mixed, preferred_element_type=jnp.float32
    )
    value_grad = value_grad + jnp.einsum(
        "bshe,bhef->bshf", key_rows, after_state, preferred_element_type=jnp.float32
    )
    query_grad = query_grad.astype(jnp.bfloat16).reshape(batch, tokens_here, width)
    key_grad = key_grad.astype(jnp.bfloat16).reshape(batch, tokens_here, width)
    value_grad = value_grad.astype(jnp.bfloat16).reshape(batch, tokens_here, width)
    grad_normed = jnp.einsum(
        "btf,df->btd", query_grad, full_query, preferred_element_type=jnp.float32
    )
    grad_normed = grad_normed + jnp.einsum(
        "btf,df->btd", key_grad, full_key, preferred_element_type=jnp.float32
    )
    grad_normed = grad_normed + jnp.einsum(
        "btf,df->btd", value_grad, full_value, preferred_element_type=jnp.float32
    )
    back = inv_rms * (
        grad_normed - normed_wide * jnp.mean(grad_normed * normed_wide, -1, keepdims=True)
    )
    grad_x_second = (grad_second.astype(jnp.float32) + back).astype(jnp.bfloat16)
    pairs = (
        (normed.reshape(-1, width), query_grad.reshape(-1, width)),
        (attn_out.reshape(-1, width), grad_first.reshape(-1, width)),
    )
    grad_query, grad_out = weight_grads(pairs, factor)
    return (x_first, grad_x_second, grad_query, grad_out)


def solution(mesh):
    placed = (
        P("dp", "ctx", None),
        P("dp", "ctx", None),
        P("dp", "ctx", None),
        P("dp", "ctx", None),
        P("dp", None),
        P("dp", None),
        P("dp", None),
        P("dp", None),
    )
    return jax.shard_map(
        on_device,
        mesh=mesh,
        in_specs=placed,
        out_specs=(
            P("dp", "ctx", None),
            P("dp", "ctx", None),
            P(("dp", "ctx"), None),
            P(("dp", "ctx"), None),
        ),
        check_vma=False,
    )
```

```python
import jax
import jax.numpy as jnp
from jax import lax
from jax.sharding import Mesh, PartitionSpec as P

HEADS = 8
HEAD_DIM = 128
CTX = ("cy", "core")


def scan_sum(shard, axis, reverse):
    count = lax.axis_size(axis)
    total = shard
    step = 1
    while step < count:
        if reverse:
            pairs = [(source, source - step) for source in range(step, count)]
        else:
            pairs = [(source, source + step) for source in range(count - step)]
        total = total + lax.ppermute(total, axis, pairs)
        step *= 2
    return total


def gather_rows(weights, piece):
    place = lax.axis_index(CTX)
    width = weights[0].shape[1]
    parts = [lax.dynamic_slice_in_dim(weight, place * piece, piece, 0) for weight in weights]
    joined = jnp.concatenate(parts, 0)
    across = lax.all_gather(joined, "dp", axis=0, tiled=False)
    return across.reshape(across.shape[0], len(weights), piece, width)


def spread_rows(across):
    blocks, count, piece, width = across.shape
    gathered = lax.all_gather(across, CTX, axis=0, tiled=False)
    gathered = jnp.transpose(gathered, (2, 1, 0, 3, 4))
    return tuple(
        gathered[index].reshape(-1, width) for index in range(count)
    )


def weight_grads(pairs, factor):
    width = pairs[0][0].shape[1]
    outer, chips, cores = lax.axis_size("dp"), lax.axis_size("cy"), lax.axis_size("core")
    mine = lax.axis_index("core")
    swap = [(0, 1), (1, 0)]
    blocks = []
    for left, right in pairs:
        other_left, other_right = lax.ppermute((left, right), "core", swap)
        both_left = jnp.concatenate([left, other_left], 0)
        both_right = jnp.concatenate([right, other_right], 0)
        tokens = both_left.shape[0]
        picked = both_left.reshape(tokens, outer * chips, cores, -1)
        picked = lax.dynamic_index_in_dim(picked, mine, 2, False).reshape(tokens, -1)
        made = lax.dot_general(
            picked, both_right, (((0,), (0,)), ((), ())), preferred_element_type=jnp.float32
        )
        blocks.append((factor * made).reshape(outer, chips, -1, width))
    rows = blocks[0].shape[2]
    stacked = jnp.concatenate(blocks, 2)
    stacked = jnp.transpose(stacked, (1, 0, 2, 3)).reshape(-1, width)
    share = lax.psum_scatter(stacked, "cy", scatter_dimension=0, tiled=True)
    share = lax.psum_scatter(share, "dp", scatter_dimension=0, tiled=True)
    return tuple(share[index * rows : (index + 1) * rows] for index in range(len(pairs)))


def on_device(y_first, x_second, grad_first, grad_second, w_query, w_key, w_value, w_out):
    batch, tokens_here, width = y_first.shape
    owners = lax.axis_size("dp") * lax.axis_size(CTX)
    factor = float(batch * tokens_here * owners) ** (-0.5)
    piece = w_query.shape[0] // lax.axis_size(CTX)
    across = gather_rows((w_query, w_key, w_value, w_out), piece)
    full_query, full_key, full_value = spread_rows(across[:, :3])
    (full_out,) = spread_rows(across[:, 3:])
    second_wide = x_second.astype(jnp.float32)
    inv_rms = lax.rsqrt(jnp.mean(second_wide * second_wide, -1, keepdims=True) + 1e-06)
    normed_wide = second_wide * inv_rms
    normed = normed_wide.astype(jnp.bfloat16)

    def project(weight):
        made = jnp.einsum("btd,df->btf", normed, weight, preferred_element_type=jnp.float32)
        return made.astype(jnp.bfloat16).reshape(batch, tokens_here, HEADS, HEAD_DIM)

    queries = project(full_query)
    key_rows = project(full_key)
    values = project(full_value)
    local_state = jnp.einsum(
        "bthe,bthf->bhef", key_rows, values, preferred_element_type=jnp.float32
    )
    before = (scan_sum(local_state, CTX, False) - local_state).astype(jnp.bfloat16)
    causal = jnp.tril(jnp.ones((tokens_here, tokens_here), dtype=bool))
    scores = jnp.einsum("bthe,bshe->bhts", queries, key_rows, preferred_element_type=jnp.float32)
    scores = jnp.where(causal[None, None], scores, 0.0).astype(jnp.bfloat16)
    mixed = jnp.einsum("bhts,bshf->bthf", scores, values, preferred_element_type=jnp.float32)
    mixed = mixed + jnp.einsum(
        "bthe,bhef->bthf", queries, before, preferred_element_type=jnp.float32
    )
    inv_head = lax.rsqrt(jnp.mean(mixed * mixed, -1, keepdims=True) + 1e-06)
    unit = mixed * inv_head
    attn_out = unit.astype(jnp.bfloat16).reshape(batch, tokens_here, width)
    attended = jnp.einsum("btf,fd->btd", attn_out, full_out, preferred_element_type=jnp.float32)
    x_first = (y_first.astype(jnp.float32) - attended).astype(jnp.bfloat16)
    grad_unit = jnp.einsum("btd,fd->btf", grad_first, full_out, preferred_element_type=jnp.float32)
    grad_unit = grad_unit.reshape(batch, tokens_here, HEADS, HEAD_DIM)
    grad_mixed = inv_head * (grad_unit - unit * jnp.mean(grad_unit * unit, -1, keepdims=True))
    grad_mixed = grad_mixed.astype(jnp.bfloat16)
    score_grad = jnp.einsum(
        "bthf,bshf->bhts", grad_mixed, values, preferred_element_type=jnp.float32
    )
    score_grad = jnp.where(causal[None, None], score_grad, 0.0).astype(jnp.bfloat16)
    grad_local = jnp.einsum(
        "bthe,bthf->bhef", queries, grad_mixed, preferred_element_type=jnp.float32
    )
    after_state = (scan_sum(grad_local, CTX, True) - grad_local).astype(jnp.bfloat16)
    query_grad = jnp.einsum(
        "bhts,bshe->bthe", score_grad, key_rows, preferred_element_type=jnp.float32
    )
    query_grad = query_grad + jnp.einsum(
        "bthf,bhef->bthe", grad_mixed, before, preferred_element_type=jnp.float32
    )
    key_grad = jnp.einsum(
        "bhts,bthe->bshe", score_grad, queries, preferred_element_type=jnp.float32
    )
    key_grad = key_grad + jnp.einsum(
        "bshf,bhef->bshe", values, after_state, preferred_element_type=jnp.float32
    )
    value_grad = jnp.einsum(
        "bhts,bthf->bshf", scores, grad_mixed, preferred_element_type=jnp.float32
    )
    value_grad = value_grad + jnp.einsum(
        "bshe,bhef->bshf", key_rows, after_state, preferred_element_type=jnp.float32
    )
    query_grad = query_grad.astype(jnp.bfloat16).reshape(batch, tokens_here, width)
    key_grad = key_grad.astype(jnp.bfloat16).reshape(batch, tokens_here, width)
    value_grad = value_grad.astype(jnp.bfloat16).reshape(batch, tokens_here, width)
    grad_normed = jnp.einsum(
        "btf,df->btd", query_grad, full_query, preferred_element_type=jnp.float32
    )
    grad_normed = grad_normed + jnp.einsum(
        "btf,df->btd", key_grad, full_key, preferred_element_type=jnp.float32
    )
    grad_normed = grad_normed + jnp.einsum(
        "btf,df->btd", value_grad, full_value, preferred_element_type=jnp.float32
    )
    back = inv_rms * (
        grad_normed - normed_wide * jnp.mean(grad_normed * normed_wide, -1, keepdims=True)
    )
    grad_x_second = (grad_second.astype(jnp.float32) + back).astype(jnp.bfloat16)
    pairs = (
        (normed.reshape(-1, width), query_grad.reshape(-1, width)),
        (attn_out.reshape(-1, width), grad_first.reshape(-1, width)),
    )
    grad_query, grad_out = weight_grads(pairs, factor)
    return (x_first, grad_x_second, grad_query, grad_out)


def solution(mesh):
    dp, ctx = mesh.devices.shape
    fine = Mesh(mesh.devices.reshape(dp, ctx // 2, 2), ("dp", "cy", "core"))
    ctx_axes = ("cy", "core")
    rows = P("dp", ctx_axes, None)
    placed = (rows, rows, rows, rows, P("dp", None), P("dp", None), P("dp", None), P("dp", None))
    return jax.shard_map(
        on_device,
        mesh=fine,
        in_specs=placed,
        out_specs=(rows, rows, P(("dp",) + ctx_axes, None), P(("dp",) + ctx_axes, None)),
        check_vma=False,
    )
```

```python
import jax
import jax.numpy as jnp
from jax import lax
from jax.sharding import Mesh, PartitionSpec as P

HEADS = 8
HEAD_DIM = 128
CTX = ("cy", "core")


def scan_sum(shard, axis, reverse):
    count = lax.axis_size(axis)
    total = shard
    span = 1
    while span < count:
        moved = []
        for hop in range(1, 4):
            step = hop * span
            if step >= count:
                break
            if reverse:
                pairs = [(source, source - step) for source in range(step, count)]
            else:
                pairs = [(source, source + step) for source in range(count - step)]
            moved.append(lax.ppermute(total, axis, pairs))
        for part in moved:
            total = total + part
        span *= 4
    return total


def gather_rows(weights, piece):
    place = lax.axis_index(CTX)
    width = weights[0].shape[1]
    parts = [lax.dynamic_slice_in_dim(weight, place * piece, piece, 0) for weight in weights]
    joined = jnp.concatenate(parts, 0)
    across = lax.all_gather(joined, "dp", axis=0, tiled=False)
    return across.reshape(across.shape[0], len(weights), piece, width)


def spread_rows(across):
    blocks, count, piece, width = across.shape
    gathered = lax.all_gather(across, CTX, axis=0, tiled=False)
    gathered = jnp.transpose(gathered, (2, 1, 0, 3, 4))
    return tuple(
        gathered[index].reshape(-1, width) for index in range(count)
    )


def weight_grads(pairs, factor):
    width = pairs[0][0].shape[1]
    outer, chips, cores = lax.axis_size("dp"), lax.axis_size("cy"), lax.axis_size("core")
    mine = lax.axis_index("core")
    swap = [(0, 1), (1, 0)]
    blocks = []
    for left, right in pairs:
        other_left, other_right = lax.ppermute((left, right), "core", swap)
        both_left = jnp.concatenate([left, other_left], 0)
        both_right = jnp.concatenate([right, other_right], 0)
        tokens = both_left.shape[0]
        picked = both_left.reshape(tokens, outer * chips, cores, -1)
        picked = lax.dynamic_index_in_dim(picked, mine, 2, False).reshape(tokens, -1)
        made = lax.dot_general(
            picked, both_right, (((0,), (0,)), ((), ())), preferred_element_type=jnp.float32
        )
        blocks.append((factor * made).reshape(outer, chips, -1, width))
    rows = blocks[0].shape[2]
    stacked = jnp.concatenate(blocks, 2)
    stacked = jnp.transpose(stacked, (1, 0, 2, 3)).reshape(-1, width)
    share = lax.psum_scatter(stacked, "cy", scatter_dimension=0, tiled=True)
    share = lax.all_to_all(
        share.reshape(outer, -1, width), "dp", 0, 0, tiled=False
    ).sum(0)
    return tuple(share[index * rows : (index + 1) * rows] for index in range(len(pairs)))


def on_device(y_first, x_second, grad_first, grad_second, w_query, w_key, w_value, w_out):
    batch, tokens_here, width = y_first.shape
    owners = lax.axis_size("dp") * lax.axis_size(CTX)
    factor = float(batch * tokens_here * owners) ** (-0.5)
    piece = w_query.shape[0] // lax.axis_size(CTX)
    across = gather_rows((w_query, w_key, w_value, w_out), piece)
    full_query, full_key, full_value, full_out = spread_rows(across)
    second_wide = x_second.astype(jnp.float32)
    inv_rms = lax.rsqrt(jnp.mean(second_wide * second_wide, -1, keepdims=True) + 1e-06)
    normed_wide = second_wide * inv_rms
    normed = normed_wide.astype(jnp.bfloat16)

    def project(weight):
        made = jnp.einsum("btd,df->btf", normed, weight, preferred_element_type=jnp.float32)
        return made.astype(jnp.bfloat16).reshape(batch, tokens_here, HEADS, HEAD_DIM)

    queries = project(full_query)
    key_rows = project(full_key)
    values = project(full_value)
    local_state = jnp.einsum(
        "bthe,bthf->bhef", key_rows, values, preferred_element_type=jnp.float32
    )
    before = (scan_sum(local_state, CTX, False) - local_state).astype(jnp.bfloat16)
    causal = jnp.tril(jnp.ones((tokens_here, tokens_here), dtype=bool))
    scores = jnp.einsum("bthe,bshe->bhts", queries, key_rows, preferred_element_type=jnp.float32)
    scores = jnp.where(causal[None, None], scores, 0.0).astype(jnp.bfloat16)
    mixed = jnp.einsum("bhts,bshf->bthf", scores, values, preferred_element_type=jnp.float32)
    mixed = mixed + jnp.einsum(
        "bthe,bhef->bthf", queries, before, preferred_element_type=jnp.float32
    )
    inv_head = lax.rsqrt(jnp.mean(mixed * mixed, -1, keepdims=True) + 1e-06)
    unit = mixed * inv_head
    attn_out = unit.astype(jnp.bfloat16).reshape(batch, tokens_here, width)
    attended = jnp.einsum("btf,fd->btd", attn_out, full_out, preferred_element_type=jnp.float32)
    x_first = (y_first.astype(jnp.float32) - attended).astype(jnp.bfloat16)
    grad_unit = jnp.einsum("btd,fd->btf", grad_first, full_out, preferred_element_type=jnp.float32)
    grad_unit = grad_unit.reshape(batch, tokens_here, HEADS, HEAD_DIM)
    grad_mixed = inv_head * (grad_unit - unit * jnp.mean(grad_unit * unit, -1, keepdims=True))
    grad_mixed = grad_mixed.astype(jnp.bfloat16)
    score_grad = jnp.einsum(
        "bthf,bshf->bhts", grad_mixed, values, preferred_element_type=jnp.float32
    )
    score_grad = jnp.where(causal[None, None], score_grad, 0.0).astype(jnp.bfloat16)
    grad_local = jnp.einsum(
        "bthe,bthf->bhef", queries, grad_mixed, preferred_element_type=jnp.float32
    )
    after_state = (scan_sum(grad_local, CTX, True) - grad_local).astype(jnp.bfloat16)
    query_grad = jnp.einsum(
        "bhts,bshe->bthe", score_grad, key_rows, preferred_element_type=jnp.float32
    )
    query_grad = query_grad + jnp.einsum(
        "bthf,bhef->bthe", grad_mixed, before, preferred_element_type=jnp.float32
    )
    key_grad = jnp.einsum(
        "bhts,bthe->bshe", score_grad, queries, preferred_element_type=jnp.float32
    )
    key_grad = key_grad + jnp.einsum(
        "bshf,bhef->bshe", values, after_state, preferred_element_type=jnp.float32
    )
    value_grad = jnp.einsum(
        "bhts,bthf->bshf", scores, grad_mixed, preferred_element_type=jnp.float32
    )
    value_grad = value_grad + jnp.einsum(
        "bshe,bhef->bshf", key_rows, after_state, preferred_element_type=jnp.float32
    )
    query_grad = query_grad.astype(jnp.bfloat16).reshape(batch, tokens_here, width)
    key_grad = key_grad.astype(jnp.bfloat16).reshape(batch, tokens_here, width)
    value_grad = value_grad.astype(jnp.bfloat16).reshape(batch, tokens_here, width)
    grad_normed = jnp.einsum(
        "btf,df->btd", query_grad, full_query, preferred_element_type=jnp.float32
    )
    grad_normed = grad_normed + jnp.einsum(
        "btf,df->btd", key_grad, full_key, preferred_element_type=jnp.float32
    )
    grad_normed = grad_normed + jnp.einsum(
        "btf,df->btd", value_grad, full_value, preferred_element_type=jnp.float32
    )
    back = inv_rms * (
        grad_normed - normed_wide * jnp.mean(grad_normed * normed_wide, -1, keepdims=True)
    )
    grad_x_second = (grad_second.astype(jnp.float32) + back).astype(jnp.bfloat16)
    pairs = (
        (normed.reshape(-1, width), query_grad.reshape(-1, width)),
        (attn_out.reshape(-1, width), grad_first.reshape(-1, width)),
    )
    grad_query, grad_out = weight_grads(pairs, factor)
    return (x_first, grad_x_second, grad_query, grad_out)


def solution(mesh):
    dp, ctx = mesh.devices.shape
    fine = Mesh(mesh.devices.reshape(dp, ctx // 2, 2), ("dp", "cy", "core"))
    ctx_axes = ("cy", "core")
    rows = P("dp", ctx_axes, None)
    placed = (rows, rows, rows, rows, P("dp", None), P("dp", None), P("dp", None), P("dp", None))
    return jax.shard_map(
        on_device,
        mesh=fine,
        in_specs=placed,
        out_specs=(rows, rows, P(("dp",) + ctx_axes, None), P(("dp",) + ctx_axes, None)),
        check_vma=False,
    )
```

```python
import jax
import jax.numpy as jnp
from jax import lax
from jax.sharding import Mesh, PartitionSpec as P

HEADS = 8
HEAD_DIM = 128
CTX = ("cy", "core")


def state_sum(shard, axis, later):
    count = lax.axis_size(axis)
    place = lax.axis_index(axis)
    gathered = lax.all_gather(shard, axis, axis=0, tiled=False)
    blocks = lax.broadcasted_iota(jnp.int32, (count,) + (1,) * shard.ndim, 0)
    chosen = blocks > place if later else blocks < place
    return jnp.sum(jnp.where(chosen, gathered, 0.0), axis=0)


def gather_rows(weights, piece):
    place = lax.axis_index(CTX)
    width = weights[0].shape[1]
    parts = [lax.dynamic_slice_in_dim(weight, place * piece, piece, 0) for weight in weights]
    joined = jnp.concatenate(parts, 0)
    across = lax.all_gather(joined, "dp", axis=0, tiled=False)
    return across.reshape(across.shape[0], len(weights), piece, width)


def spread_rows(across):
    blocks, count, piece, width = across.shape
    gathered = lax.all_gather(across, CTX, axis=0, tiled=False)
    gathered = jnp.transpose(gathered, (2, 1, 0, 3, 4))
    return tuple(
        gathered[index].reshape(-1, width) for index in range(count)
    )


def weight_grads(pairs, factor):
    width = pairs[0][0].shape[1]
    outer, chips, cores = lax.axis_size("dp"), lax.axis_size("cy"), lax.axis_size("core")
    mine = lax.axis_index("core")
    swap = [(0, 1), (1, 0)]
    blocks = []
    for left, right in pairs:
        other_left, other_right = lax.ppermute((left, right), "core", swap)
        both_left = jnp.concatenate([left, other_left], 0)
        both_right = jnp.concatenate([right, other_right], 0)
        tokens = both_left.shape[0]
        picked = both_left.reshape(tokens, outer * chips, cores, -1)
        picked = lax.dynamic_index_in_dim(picked, mine, 2, False).reshape(tokens, -1)
        made = lax.dot_general(
            picked, both_right, (((0,), (0,)), ((), ())), preferred_element_type=jnp.float32
        )
        blocks.append((factor * made).reshape(outer, chips, -1, width))
    rows = blocks[0].shape[2]
    stacked = jnp.concatenate(blocks, 2)
    stacked = jnp.transpose(stacked, (1, 0, 2, 3)).reshape(-1, width)
    share = lax.all_to_all(
        stacked.reshape(chips, -1, width), "cy", 0, 0, tiled=False
    ).sum(0)
    share = lax.all_to_all(
        share.reshape(outer, -1, width), "dp", 0, 0, tiled=False
    ).sum(0)
    return tuple(share[index * rows : (index + 1) * rows] for index in range(len(pairs)))


def on_device(y_first, x_second, grad_first, grad_second, w_query, w_key, w_value, w_out):
    batch, tokens_here, width = y_first.shape
    owners = lax.axis_size("dp") * lax.axis_size(CTX)
    factor = float(batch * tokens_here * owners) ** (-0.5)
    piece = w_query.shape[0] // lax.axis_size(CTX)
    across = gather_rows((w_query, w_key, w_value, w_out), piece)
    full_query, full_key, full_value, full_out = spread_rows(across)
    second_wide = x_second.astype(jnp.float32)
    inv_rms = lax.rsqrt(jnp.mean(second_wide * second_wide, -1, keepdims=True) + 1e-06)
    normed_wide = second_wide * inv_rms
    normed = normed_wide.astype(jnp.bfloat16)

    def project(weight):
        made = jnp.einsum("btd,df->btf", normed, weight, preferred_element_type=jnp.float32)
        return made.astype(jnp.bfloat16).reshape(batch, tokens_here, HEADS, HEAD_DIM)

    queries = project(full_query)
    key_rows = project(full_key)
    values = project(full_value)
    local_state = jnp.einsum(
        "bthe,bthf->bhef", key_rows, values, preferred_element_type=jnp.float32
    )
    before = state_sum(local_state, CTX, False).astype(jnp.bfloat16)
    causal = jnp.tril(jnp.ones((tokens_here, tokens_here), dtype=bool))
    scores = jnp.einsum("bthe,bshe->bhts", queries, key_rows, preferred_element_type=jnp.float32)
    scores = jnp.where(causal[None, None], scores, 0.0).astype(jnp.bfloat16)
    mixed = jnp.einsum("bhts,bshf->bthf", scores, values, preferred_element_type=jnp.float32)
    mixed = mixed + jnp.einsum(
        "bthe,bhef->bthf", queries, before, preferred_element_type=jnp.float32
    )
    inv_head = lax.rsqrt(jnp.mean(mixed * mixed, -1, keepdims=True) + 1e-06)
    unit = mixed * inv_head
    attn_out = unit.astype(jnp.bfloat16).reshape(batch, tokens_here, width)
    attended = jnp.einsum("btf,fd->btd", attn_out, full_out, preferred_element_type=jnp.float32)
    x_first = (y_first.astype(jnp.float32) - attended).astype(jnp.bfloat16)
    grad_unit = jnp.einsum("btd,fd->btf", grad_first, full_out, preferred_element_type=jnp.float32)
    grad_unit = grad_unit.reshape(batch, tokens_here, HEADS, HEAD_DIM)
    grad_mixed = inv_head * (grad_unit - unit * jnp.mean(grad_unit * unit, -1, keepdims=True))
    grad_mixed = grad_mixed.astype(jnp.bfloat16)
    score_grad = jnp.einsum(
        "bthf,bshf->bhts", grad_mixed, values, preferred_element_type=jnp.float32
    )
    score_grad = jnp.where(causal[None, None], score_grad, 0.0).astype(jnp.bfloat16)
    grad_local = jnp.einsum(
        "bthe,bthf->bhef", queries, grad_mixed, preferred_element_type=jnp.float32
    )
    after_state = state_sum(grad_local, CTX, True).astype(jnp.bfloat16)
    query_grad = jnp.einsum(
        "bhts,bshe->bthe", score_grad, key_rows, preferred_element_type=jnp.float32
    )
    query_grad = query_grad + jnp.einsum(
        "bthf,bhef->bthe", grad_mixed, before, preferred_element_type=jnp.float32
    )
    key_grad = jnp.einsum(
        "bhts,bthe->bshe", score_grad, queries, preferred_element_type=jnp.float32
    )
    key_grad = key_grad + jnp.einsum(
        "bshf,bhef->bshe", values, after_state, preferred_element_type=jnp.float32
    )
    value_grad = jnp.einsum(
        "bhts,bthf->bshf", scores, grad_mixed, preferred_element_type=jnp.float32
    )
    value_grad = value_grad + jnp.einsum(
        "bshe,bhef->bshf", key_rows, after_state, preferred_element_type=jnp.float32
    )
    query_grad = query_grad.astype(jnp.bfloat16).reshape(batch, tokens_here, width)
    key_grad = key_grad.astype(jnp.bfloat16).reshape(batch, tokens_here, width)
    value_grad = value_grad.astype(jnp.bfloat16).reshape(batch, tokens_here, width)
    grad_normed = jnp.einsum(
        "btf,df->btd", query_grad, full_query, preferred_element_type=jnp.float32
    )
    grad_normed = grad_normed + jnp.einsum(
        "btf,df->btd", key_grad, full_key, preferred_element_type=jnp.float32
    )
    grad_normed = grad_normed + jnp.einsum(
        "btf,df->btd", value_grad, full_value, preferred_element_type=jnp.float32
    )
    back = inv_rms * (
        grad_normed - normed_wide * jnp.mean(grad_normed * normed_wide, -1, keepdims=True)
    )
    grad_x_second = (grad_second.astype(jnp.float32) + back).astype(jnp.bfloat16)
    pairs = (
        (normed.reshape(-1, width), query_grad.reshape(-1, width)),
        (attn_out.reshape(-1, width), grad_first.reshape(-1, width)),
    )
    grad_query, grad_out = weight_grads(pairs, factor)
    return (x_first, grad_x_second, grad_query, grad_out)


def solution(mesh):
    dp, ctx = mesh.devices.shape
    fine = Mesh(mesh.devices.reshape(dp, ctx // 2, 2), ("dp", "cy", "core"))
    ctx_axes = ("cy", "core")
    rows = P("dp", ctx_axes, None)
    placed = (rows, rows, rows, rows, P("dp", None), P("dp", None), P("dp", None), P("dp", None))
    return jax.shard_map(
        on_device,
        mesh=fine,
        in_specs=placed,
        out_specs=(rows, rows, P(("dp",) + ctx_axes, None), P(("dp",) + ctx_axes, None)),
        check_vma=False,
    )
```

```python
import jax
import jax.numpy as jnp
from jax import lax
from jax.sharding import Mesh, PartitionSpec as P

HEADS = 8
HEAD_DIM = 128
CTX = ("cy", "core")


def state_sum(shard, later):
    chips = lax.axis_size("cy")
    chip = lax.axis_index("cy")
    core = lax.axis_index("core")
    swap = [(0, 1), (1, 0)]
    partner = lax.ppermute(shard, "core", swap)
    both = shard + partner
    half = shard.shape[1] // 2
    mine = lax.dynamic_slice_in_dim(both, core * half, half, 1)
    gathered = lax.all_gather(mine, "cy", axis=0, tiled=False)
    blocks = lax.broadcasted_iota(jnp.int32, (chips,) + (1,) * mine.ndim, 0)
    chosen = blocks > chip if later else blocks < chip
    summed = jnp.sum(jnp.where(chosen, gathered, 0.0), axis=0)
    other = lax.ppermute(summed, "core", swap)
    first = jnp.where(core == 0, summed, other)
    second = jnp.where(core == 0, other, summed)
    across = jnp.concatenate([first, second], 1)
    inside = (core == 0) if later else (core == 1)
    return across + jnp.where(inside, partner, 0.0)


def gather_rows(weights, piece):
    place = lax.axis_index(CTX)
    width = weights[0].shape[1]
    parts = [lax.dynamic_slice_in_dim(weight, place * piece, piece, 0) for weight in weights]
    joined = jnp.concatenate(parts, 0)
    across = lax.all_gather(joined, "dp", axis=0, tiled=False)
    return across.reshape(across.shape[0], len(weights), piece, width)


def spread_rows(across):
    blocks, count, piece, width = across.shape
    gathered = lax.all_gather(across, CTX, axis=0, tiled=False)
    gathered = jnp.transpose(gathered, (2, 1, 0, 3, 4))
    return tuple(
        gathered[index].reshape(-1, width) for index in range(count)
    )


def weight_grads(pairs, factor):
    width = pairs[0][0].shape[1]
    outer, chips, cores = lax.axis_size("dp"), lax.axis_size("cy"), lax.axis_size("core")
    mine = lax.axis_index("core")
    swap = [(0, 1), (1, 0)]
    blocks = []
    for left, right in pairs:
        other_left, other_right = lax.ppermute((left, right), "core", swap)
        both_left = jnp.concatenate([left, other_left], 0)
        both_right = jnp.concatenate([right, other_right], 0)
        tokens = both_left.shape[0]
        picked = both_left.reshape(tokens, outer * chips, cores, -1)
        picked = lax.dynamic_index_in_dim(picked, mine, 2, False).reshape(tokens, -1)
        made = lax.dot_general(
            picked, both_right, (((0,), (0,)), ((), ())), preferred_element_type=jnp.float32
        )
        blocks.append((factor * made).reshape(outer, chips, -1, width))
    rows = blocks[0].shape[2]
    stacked = jnp.concatenate(blocks, 2)
    stacked = jnp.transpose(stacked, (1, 0, 2, 3)).reshape(-1, width)
    share = lax.all_to_all(
        stacked.reshape(chips, -1, width), "cy", 0, 0, tiled=False
    ).sum(0)
    share = lax.all_to_all(
        share.reshape(outer, -1, width), "dp", 0, 0, tiled=False
    ).sum(0)
    return tuple(share[index * rows : (index + 1) * rows] for index in range(len(pairs)))


def on_device(y_first, x_second, grad_first, grad_second, w_query, w_key, w_value, w_out):
    batch, tokens_here, width = y_first.shape
    owners = lax.axis_size("dp") * lax.axis_size(CTX)
    factor = float(batch * tokens_here * owners) ** (-0.5)
    piece = w_query.shape[0] // lax.axis_size(CTX)
    across = gather_rows((w_query, w_key, w_value, w_out), piece)
    full_query, full_key, full_value, full_out = spread_rows(across)
    second_wide = x_second.astype(jnp.float32)
    inv_rms = lax.rsqrt(jnp.mean(second_wide * second_wide, -1, keepdims=True) + 1e-06)
    normed_wide = second_wide * inv_rms
    normed = normed_wide.astype(jnp.bfloat16)

    def project(weight):
        made = jnp.einsum("btd,df->btf", normed, weight, preferred_element_type=jnp.float32)
        return made.astype(jnp.bfloat16).reshape(batch, tokens_here, HEADS, HEAD_DIM)

    queries = project(full_query)
    key_rows = project(full_key)
    values = project(full_value)
    local_state = jnp.einsum(
        "bthe,bthf->bhef", key_rows, values, preferred_element_type=jnp.float32
    )
    before = state_sum(local_state, False).astype(jnp.bfloat16)
    causal = jnp.tril(jnp.ones((tokens_here, tokens_here), dtype=bool))
    scores = jnp.einsum("bthe,bshe->bhts", queries, key_rows, preferred_element_type=jnp.float32)
    scores = jnp.where(causal[None, None], scores, 0.0).astype(jnp.bfloat16)
    mixed = jnp.einsum("bhts,bshf->bthf", scores, values, preferred_element_type=jnp.float32)
    mixed = mixed + jnp.einsum(
        "bthe,bhef->bthf", queries, before, preferred_element_type=jnp.float32
    )
    inv_head = lax.rsqrt(jnp.mean(mixed * mixed, -1, keepdims=True) + 1e-06)
    unit = mixed * inv_head
    attn_out = unit.astype(jnp.bfloat16).reshape(batch, tokens_here, width)
    attended = jnp.einsum("btf,fd->btd", attn_out, full_out, preferred_element_type=jnp.float32)
    x_first = (y_first.astype(jnp.float32) - attended).astype(jnp.bfloat16)
    grad_unit = jnp.einsum("btd,fd->btf", grad_first, full_out, preferred_element_type=jnp.float32)
    grad_unit = grad_unit.reshape(batch, tokens_here, HEADS, HEAD_DIM)
    grad_mixed = inv_head * (grad_unit - unit * jnp.mean(grad_unit * unit, -1, keepdims=True))
    grad_mixed = grad_mixed.astype(jnp.bfloat16)
    score_grad = jnp.einsum(
        "bthf,bshf->bhts", grad_mixed, values, preferred_element_type=jnp.float32
    )
    score_grad = jnp.where(causal[None, None], score_grad, 0.0).astype(jnp.bfloat16)
    grad_local = jnp.einsum(
        "bthe,bthf->bhef", queries, grad_mixed, preferred_element_type=jnp.float32
    )
    after_state = state_sum(grad_local, True).astype(jnp.bfloat16)
    query_grad = jnp.einsum(
        "bhts,bshe->bthe", score_grad, key_rows, preferred_element_type=jnp.float32
    )
    query_grad = query_grad + jnp.einsum(
        "bthf,bhef->bthe", grad_mixed, before, preferred_element_type=jnp.float32
    )
    key_grad = jnp.einsum(
        "bhts,bthe->bshe", score_grad, queries, preferred_element_type=jnp.float32
    )
    key_grad = key_grad + jnp.einsum(
        "bshf,bhef->bshe", values, after_state, preferred_element_type=jnp.float32
    )
    value_grad = jnp.einsum(
        "bhts,bthf->bshf", scores, grad_mixed, preferred_element_type=jnp.float32
    )
    value_grad = value_grad + jnp.einsum(
        "bshe,bhef->bshf", key_rows, after_state, preferred_element_type=jnp.float32
    )
    query_grad = query_grad.astype(jnp.bfloat16).reshape(batch, tokens_here, width)
    key_grad = key_grad.astype(jnp.bfloat16).reshape(batch, tokens_here, width)
    value_grad = value_grad.astype(jnp.bfloat16).reshape(batch, tokens_here, width)
    grad_normed = jnp.einsum(
        "btf,df->btd", query_grad, full_query, preferred_element_type=jnp.float32
    )
    grad_normed = grad_normed + jnp.einsum(
        "btf,df->btd", key_grad, full_key, preferred_element_type=jnp.float32
    )
    grad_normed = grad_normed + jnp.einsum(
        "btf,df->btd", value_grad, full_value, preferred_element_type=jnp.float32
    )
    back = inv_rms * (
        grad_normed - normed_wide * jnp.mean(grad_normed * normed_wide, -1, keepdims=True)
    )
    grad_x_second = (grad_second.astype(jnp.float32) + back).astype(jnp.bfloat16)
    pairs = (
        (normed.reshape(-1, width), query_grad.reshape(-1, width)),
        (attn_out.reshape(-1, width), grad_first.reshape(-1, width)),
    )
    grad_query, grad_out = weight_grads(pairs, factor)
    return (x_first, grad_x_second, grad_query, grad_out)


def solution(mesh):
    dp, ctx = mesh.devices.shape
    fine = Mesh(mesh.devices.reshape(dp, ctx // 2, 2), ("dp", "cy", "core"))
    ctx_axes = ("cy", "core")
    rows = P("dp", ctx_axes, None)
    placed = (rows, rows, rows, rows, P("dp", None), P("dp", None), P("dp", None), P("dp", None))
    return jax.shard_map(
        on_device,
        mesh=fine,
        in_specs=placed,
        out_specs=(rows, rows, P(("dp",) + ctx_axes, None), P(("dp",) + ctx_axes, None)),
        check_vma=False,
    )
```

```python
import jax
import jax.numpy as jnp
from jax import lax
from jax.sharding import Mesh, PartitionSpec as P

HEADS = 8
HEAD_DIM = 128
CTX = ("cy", "core")


def state_sum(shard, later):
    chips = lax.axis_size("cy")
    chip = lax.axis_index("cy")
    core = lax.axis_index("core")
    swap = [(0, 1), (1, 0)]
    partner = lax.ppermute(shard, "core", swap)
    both = shard + partner
    half = shard.shape[1] // 2
    mine = lax.dynamic_slice_in_dim(both, core * half, half, 1)
    gathered = lax.all_gather(mine, "cy", axis=0, tiled=False)
    blocks = lax.broadcasted_iota(jnp.int32, (chips,) + (1,) * mine.ndim, 0)
    chosen = blocks > chip if later else blocks < chip
    summed = jnp.sum(jnp.where(chosen, gathered, 0.0), axis=0)
    other = lax.ppermute(summed, "core", swap)
    first = jnp.where(core == 0, summed, other)
    second = jnp.where(core == 0, other, summed)
    across = jnp.concatenate([first, second], 1)
    inside = (core == 0) if later else (core == 1)
    return across + jnp.where(inside, partner, 0.0)


def gather_rows(weights, piece):
    place = lax.axis_index(CTX)
    width = weights[0].shape[1]
    parts = [lax.dynamic_slice_in_dim(weight, place * piece, piece, 0) for weight in weights]
    joined = jnp.concatenate(parts, 0)
    copies = jnp.broadcast_to(joined[None], (lax.axis_size("dp"),) + joined.shape)
    across = lax.all_to_all(copies, "dp", 0, 0, tiled=False)
    return across.reshape(across.shape[0], len(weights), piece, width)


def spread_rows(across):
    blocks, count, piece, width = across.shape
    gathered = lax.all_gather(across, CTX, axis=0, tiled=False)
    gathered = jnp.transpose(gathered, (2, 1, 0, 3, 4))
    return tuple(
        gathered[index].reshape(-1, width) for index in range(count)
    )


def weight_grads(pairs, factor, wait_for):
    width = pairs[0][0].shape[1]
    outer, chips, cores = lax.axis_size("dp"), lax.axis_size("cy"), lax.axis_size("core")
    mine = lax.axis_index("core")
    swap = [(0, 1), (1, 0)]
    blocks = []
    for left, right in pairs:
        other_left, other_right = lax.ppermute((left, right), "core", swap)
        both_left = jnp.concatenate([left, other_left], 0)
        both_right = jnp.concatenate([right, other_right], 0)
        tokens = both_left.shape[0]
        picked = both_left.reshape(tokens, outer * chips, cores, -1)
        picked = lax.dynamic_index_in_dim(picked, mine, 2, False).reshape(tokens, -1)
        made = lax.dot_general(
            picked, both_right, (((0,), (0,)), ((), ())), preferred_element_type=jnp.float32
        )
        blocks.append((factor * made).reshape(outer, chips, -1, width))
    rows = blocks[0].shape[2]
    stacked = jnp.concatenate(blocks, 2)
    stacked = jnp.transpose(stacked, (1, 0, 2, 3)).reshape(-1, width)
    stacked, _ = lax.optimization_barrier((stacked, wait_for))
    share = lax.all_to_all(
        stacked.reshape(chips, -1, width), "cy", 0, 0, tiled=False
    ).sum(0)
    share = lax.all_to_all(
        share.reshape(outer, -1, width), "dp", 0, 0, tiled=False
    ).sum(0)
    return tuple(share[index * rows : (index + 1) * rows] for index in range(len(pairs)))


def on_device(y_first, x_second, grad_first, grad_second, w_query, w_key, w_value, w_out):
    batch, tokens_here, width = y_first.shape
    owners = lax.axis_size("dp") * lax.axis_size(CTX)
    factor = float(batch * tokens_here * owners) ** (-0.5)
    piece = w_query.shape[0] // lax.axis_size(CTX)
    across = gather_rows((w_query, w_key, w_value, w_out), piece)
    full_query, full_key, full_value, full_out = spread_rows(across)
    second_wide = x_second.astype(jnp.float32)
    inv_rms = lax.rsqrt(jnp.mean(second_wide * second_wide, -1, keepdims=True) + 1e-06)
    normed_wide = second_wide * inv_rms
    normed = normed_wide.astype(jnp.bfloat16)

    def project(weight):
        made = jnp.einsum("btd,df->btf", normed, weight, preferred_element_type=jnp.float32)
        return made.astype(jnp.bfloat16).reshape(batch, tokens_here, HEADS, HEAD_DIM)

    queries = project(full_query)
    key_rows = project(full_key)
    values = project(full_value)
    local_state = jnp.einsum(
        "bthe,bthf->bhef", key_rows, values, preferred_element_type=jnp.float32
    )
    before = state_sum(local_state, False).astype(jnp.bfloat16)
    causal = jnp.tril(jnp.ones((tokens_here, tokens_here), dtype=bool))
    scores = jnp.einsum("bthe,bshe->bhts", queries, key_rows, preferred_element_type=jnp.float32)
    scores = jnp.where(causal[None, None], scores, 0.0).astype(jnp.bfloat16)
    mixed = jnp.einsum("bhts,bshf->bthf", scores, values, preferred_element_type=jnp.float32)
    mixed = mixed + jnp.einsum(
        "bthe,bhef->bthf", queries, before, preferred_element_type=jnp.float32
    )
    inv_head = lax.rsqrt(jnp.mean(mixed * mixed, -1, keepdims=True) + 1e-06)
    unit = mixed * inv_head
    attn_out = unit.astype(jnp.bfloat16).reshape(batch, tokens_here, width)
    attended = jnp.einsum("btf,fd->btd", attn_out, full_out, preferred_element_type=jnp.float32)
    x_first = (y_first.astype(jnp.float32) - attended).astype(jnp.bfloat16)
    grad_unit = jnp.einsum("btd,fd->btf", grad_first, full_out, preferred_element_type=jnp.float32)
    grad_unit = grad_unit.reshape(batch, tokens_here, HEADS, HEAD_DIM)
    grad_mixed = inv_head * (grad_unit - unit * jnp.mean(grad_unit * unit, -1, keepdims=True))
    grad_mixed = grad_mixed.astype(jnp.bfloat16)
    score_grad = jnp.einsum(
        "bthf,bshf->bhts", grad_mixed, values, preferred_element_type=jnp.float32
    )
    score_grad = jnp.where(causal[None, None], score_grad, 0.0).astype(jnp.bfloat16)
    grad_local = jnp.einsum(
        "bthe,bthf->bhef", queries, grad_mixed, preferred_element_type=jnp.float32
    )
    after_state = state_sum(grad_local, True).astype(jnp.bfloat16)
    query_grad = jnp.einsum(
        "bhts,bshe->bthe", score_grad, key_rows, preferred_element_type=jnp.float32
    )
    query_grad = query_grad + jnp.einsum(
        "bthf,bhef->bthe", grad_mixed, before, preferred_element_type=jnp.float32
    )
    key_grad = jnp.einsum(
        "bhts,bthe->bshe", score_grad, queries, preferred_element_type=jnp.float32
    )
    key_grad = key_grad + jnp.einsum(
        "bshf,bhef->bshe", values, after_state, preferred_element_type=jnp.float32
    )
    value_grad = jnp.einsum(
        "bhts,bthf->bshf", scores, grad_mixed, preferred_element_type=jnp.float32
    )
    value_grad = value_grad + jnp.einsum(
        "bshe,bhef->bshf", key_rows, after_state, preferred_element_type=jnp.float32
    )
    query_grad = query_grad.astype(jnp.bfloat16).reshape(batch, tokens_here, width)
    key_grad = key_grad.astype(jnp.bfloat16).reshape(batch, tokens_here, width)
    value_grad = value_grad.astype(jnp.bfloat16).reshape(batch, tokens_here, width)
    grad_normed = jnp.einsum(
        "btf,df->btd", query_grad, full_query, preferred_element_type=jnp.float32
    )
    grad_normed = grad_normed + jnp.einsum(
        "btf,df->btd", key_grad, full_key, preferred_element_type=jnp.float32
    )
    grad_normed = grad_normed + jnp.einsum(
        "btf,df->btd", value_grad, full_value, preferred_element_type=jnp.float32
    )
    back = inv_rms * (
        grad_normed - normed_wide * jnp.mean(grad_normed * normed_wide, -1, keepdims=True)
    )
    grad_x_second = (grad_second.astype(jnp.float32) + back).astype(jnp.bfloat16)
    pairs = (
        (normed.reshape(-1, width), query_grad.reshape(-1, width)),
        (attn_out.reshape(-1, width), grad_first.reshape(-1, width)),
    )
    grad_query, grad_out = weight_grads(pairs, factor, after_state)
    return (x_first, grad_x_second, grad_query, grad_out)


def solution(mesh):
    dp, ctx = mesh.devices.shape
    fine = Mesh(mesh.devices.reshape(dp, ctx // 2, 2), ("dp", "cy", "core"))
    ctx_axes = ("cy", "core")
    rows = P("dp", ctx_axes, None)
    placed = (rows, rows, rows, rows, P("dp", None), P("dp", None), P("dp", None), P("dp", None))
    return jax.shard_map(
        on_device,
        mesh=fine,
        in_specs=placed,
        out_specs=(rows, rows, P(("dp",) + ctx_axes, None), P(("dp",) + ctx_axes, None)),
        check_vma=False,
    )
```

```python
import jax
import jax.numpy as jnp
from jax import lax
from jax.sharding import Mesh, PartitionSpec as P

HEADS = 8
HEAD_DIM = 128
CTX = ("cy", "core")


def state_sum(shard, later):
    chips = lax.axis_size("cy")
    chip = lax.axis_index("cy")
    core = lax.axis_index("core")
    swap = [(0, 1), (1, 0)]
    partner = lax.ppermute(shard, "core", swap)
    both = shard + partner
    half = shard.shape[1] // 2
    mine = lax.dynamic_slice_in_dim(both, core * half, half, 1)
    gathered = lax.all_gather(mine, "cy", axis=0, tiled=False)
    blocks = lax.broadcasted_iota(jnp.int32, (chips,) + (1,) * mine.ndim, 0)
    chosen = blocks > chip if later else blocks < chip
    summed = jnp.sum(jnp.where(chosen, gathered, 0.0), axis=0)
    other = lax.ppermute(summed, "core", swap)
    first = jnp.where(core == 0, summed, other)
    second = jnp.where(core == 0, other, summed)
    across = jnp.concatenate([first, second], 1)
    inside = (core == 0) if later else (core == 1)
    return across + jnp.where(inside, partner, 0.0)


def gather_rows(weights, piece):
    place = lax.axis_index(CTX)
    width = weights[0].shape[1]
    parts = [lax.dynamic_slice_in_dim(weight, place * piece, piece, 0) for weight in weights]
    joined = jnp.concatenate(parts, 0)
    copies = jnp.broadcast_to(joined[None], (lax.axis_size("dp"),) + joined.shape)
    across = lax.all_to_all(copies, "dp", 0, 0, tiled=False)
    return across.reshape(across.shape[0], len(weights), piece, width)


def spread_rows(across):
    blocks, count, piece, width = across.shape
    gathered = lax.all_gather(across, CTX, axis=0, tiled=False)
    gathered = jnp.transpose(gathered, (2, 1, 0, 3, 4))
    return tuple(
        gathered[index].reshape(-1, width) for index in range(count)
    )


def weight_grads(pairs, factor, wait_for):
    width = pairs[0][0].shape[1]
    outer, chips, cores = lax.axis_size("dp"), lax.axis_size("cy"), lax.axis_size("core")
    mine = lax.axis_index("core")
    swap = [(0, 1), (1, 0)]
    blocks = []
    for left, right in pairs:
        other_left, other_right = lax.ppermute((left, right), "core", swap)
        both_left = jnp.concatenate([left, other_left], 0)
        both_right = jnp.concatenate([right, other_right], 0)
        tokens = both_left.shape[0]
        picked = both_left.reshape(tokens, outer * chips, cores, -1)
        picked = lax.dynamic_index_in_dim(picked, mine, 2, False).reshape(tokens, -1)
        made = lax.dot_general(
            picked, both_right, (((0,), (0,)), ((), ())), preferred_element_type=jnp.float32
        )
        blocks.append((factor * made).reshape(outer, chips, -1, width))
    rows = blocks[0].shape[2]
    stacked = jnp.concatenate(blocks, 2)
    stacked = jnp.transpose(stacked, (1, 0, 2, 3)).reshape(-1, width)
    stacked, _ = lax.optimization_barrier((stacked, wait_for))
    share = lax.all_to_all(
        stacked.reshape(chips, -1, width).astype(jnp.bfloat16), "cy", 0, 0, tiled=False
    ).astype(jnp.float32).sum(0)
    share = lax.all_to_all(
        share.reshape(outer, -1, width), "dp", 0, 0, tiled=False
    ).sum(0)
    return tuple(share[index * rows : (index + 1) * rows] for index in range(len(pairs)))


def on_device(y_first, x_second, grad_first, grad_second, w_query, w_key, w_value, w_out):
    batch, tokens_here, width = y_first.shape
    owners = lax.axis_size("dp") * lax.axis_size(CTX)
    factor = float(batch * tokens_here * owners) ** (-0.5)
    piece = w_query.shape[0] // lax.axis_size(CTX)
    across = gather_rows((w_query, w_key, w_value, w_out), piece)
    full_query, full_key, full_value, full_out = spread_rows(across)
    second_wide = x_second.astype(jnp.float32)
    inv_rms = lax.rsqrt(jnp.mean(second_wide * second_wide, -1, keepdims=True) + 1e-06)
    normed_wide = second_wide * inv_rms
    normed = normed_wide.astype(jnp.bfloat16)

    def project(weight):
        made = jnp.einsum("btd,df->btf", normed, weight, preferred_element_type=jnp.float32)
        return made.astype(jnp.bfloat16).reshape(batch, tokens_here, HEADS, HEAD_DIM)

    queries = project(full_query)
    key_rows = project(full_key)
    values = project(full_value)
    local_state = jnp.einsum(
        "bthe,bthf->bhef", key_rows, values, preferred_element_type=jnp.float32
    )
    before = state_sum(local_state, False).astype(jnp.bfloat16)
    causal = jnp.tril(jnp.ones((tokens_here, tokens_here), dtype=bool))
    scores = jnp.einsum("bthe,bshe->bhts", queries, key_rows, preferred_element_type=jnp.float32)
    scores = jnp.where(causal[None, None], scores, 0.0).astype(jnp.bfloat16)
    mixed = jnp.einsum("bhts,bshf->bthf", scores, values, preferred_element_type=jnp.float32)
    mixed = mixed + jnp.einsum(
        "bthe,bhef->bthf", queries, before, preferred_element_type=jnp.float32
    )
    inv_head = lax.rsqrt(jnp.mean(mixed * mixed, -1, keepdims=True) + 1e-06)
    unit = mixed * inv_head
    attn_out = unit.astype(jnp.bfloat16).reshape(batch, tokens_here, width)
    attended = jnp.einsum("btf,fd->btd", attn_out, full_out, preferred_element_type=jnp.float32)
    x_first = (y_first.astype(jnp.float32) - attended).astype(jnp.bfloat16)
    grad_unit = jnp.einsum("btd,fd->btf", grad_first, full_out, preferred_element_type=jnp.float32)
    grad_unit = grad_unit.reshape(batch, tokens_here, HEADS, HEAD_DIM)
    grad_mixed = inv_head * (grad_unit - unit * jnp.mean(grad_unit * unit, -1, keepdims=True))
    grad_mixed = grad_mixed.astype(jnp.bfloat16)
    score_grad = jnp.einsum(
        "bthf,bshf->bhts", grad_mixed, values, preferred_element_type=jnp.float32
    )
    score_grad = jnp.where(causal[None, None], score_grad, 0.0).astype(jnp.bfloat16)
    grad_local = jnp.einsum(
        "bthe,bthf->bhef", queries, grad_mixed, preferred_element_type=jnp.float32
    )
    after_state = state_sum(grad_local, True).astype(jnp.bfloat16)
    query_grad = jnp.einsum(
        "bhts,bshe->bthe", score_grad, key_rows, preferred_element_type=jnp.float32
    )
    query_grad = query_grad + jnp.einsum(
        "bthf,bhef->bthe", grad_mixed, before, preferred_element_type=jnp.float32
    )
    key_grad = jnp.einsum(
        "bhts,bthe->bshe", score_grad, queries, preferred_element_type=jnp.float32
    )
    key_grad = key_grad + jnp.einsum(
        "bshf,bhef->bshe", values, after_state, preferred_element_type=jnp.float32
    )
    value_grad = jnp.einsum(
        "bhts,bthf->bshf", scores, grad_mixed, preferred_element_type=jnp.float32
    )
    value_grad = value_grad + jnp.einsum(
        "bshe,bhef->bshf", key_rows, after_state, preferred_element_type=jnp.float32
    )
    query_grad = query_grad.astype(jnp.bfloat16).reshape(batch, tokens_here, width)
    key_grad = key_grad.astype(jnp.bfloat16).reshape(batch, tokens_here, width)
    value_grad = value_grad.astype(jnp.bfloat16).reshape(batch, tokens_here, width)
    grad_normed = jnp.einsum(
        "btf,df->btd", query_grad, full_query, preferred_element_type=jnp.float32
    )
    grad_normed = grad_normed + jnp.einsum(
        "btf,df->btd", key_grad, full_key, preferred_element_type=jnp.float32
    )
    grad_normed = grad_normed + jnp.einsum(
        "btf,df->btd", value_grad, full_value, preferred_element_type=jnp.float32
    )
    back = inv_rms * (
        grad_normed - normed_wide * jnp.mean(grad_normed * normed_wide, -1, keepdims=True)
    )
    grad_x_second = (grad_second.astype(jnp.float32) + back).astype(jnp.bfloat16)
    pairs = (
        (normed.reshape(-1, width), query_grad.reshape(-1, width)),
        (attn_out.reshape(-1, width), grad_first.reshape(-1, width)),
    )
    grad_query, grad_out = weight_grads(pairs, factor, after_state)
    return (x_first, grad_x_second, grad_query, grad_out)


def solution(mesh):
    dp, ctx = mesh.devices.shape
    fine = Mesh(mesh.devices.reshape(dp, ctx // 2, 2), ("dp", "cy", "core"))
    ctx_axes = ("cy", "core")
    rows = P("dp", ctx_axes, None)
    placed = (rows, rows, rows, rows, P("dp", None), P("dp", None), P("dp", None), P("dp", None))
    return jax.shard_map(
        on_device,
        mesh=fine,
        in_specs=placed,
        out_specs=(rows, rows, P(("dp",) + ctx_axes, None), P(("dp",) + ctx_axes, None)),
        check_vma=False,
    )
```

```python
import jax
import jax.numpy as jnp
from jax import lax
from jax.sharding import Mesh, PartitionSpec as P

HEADS = 8
HEAD_DIM = 128
CTX = ("cy", "core")


def state_sum(shard, later):
    chips = lax.axis_size("cy")
    chip = lax.axis_index("cy")
    core = lax.axis_index("core")
    swap = [(0, 1), (1, 0)]
    partner = lax.ppermute(shard, "core", swap)
    both = shard + partner
    half = shard.shape[1] // 2
    mine = lax.dynamic_slice_in_dim(both, core * half, half, 1)
    gathered = lax.all_gather(mine, "cy", axis=0, tiled=False)
    blocks = lax.broadcasted_iota(jnp.int32, (chips,) + (1,) * mine.ndim, 0)
    chosen = blocks > chip if later else blocks < chip
    summed = jnp.sum(jnp.where(chosen, gathered, 0.0), axis=0)
    other = lax.ppermute(summed, "core", swap)
    first = jnp.where(core == 0, summed, other)
    second = jnp.where(core == 0, other, summed)
    across = jnp.concatenate([first, second], 1)
    inside = (core == 0) if later else (core == 1)
    return across + jnp.where(inside, partner, 0.0)


def gather_rows(weights, piece):
    place = lax.axis_index(CTX)
    width = weights[0].shape[1]
    blocks = lax.axis_size("dp")
    parts = [lax.dynamic_slice_in_dim(weight, place * piece, piece, 0) for weight in weights]
    joined = jnp.concatenate(parts, 0)
    copies = jnp.broadcast_to(joined[None], (blocks,) + joined.shape)
    across = lax.all_to_all(copies, "dp", 0, 0, tiled=False)
    across = across.reshape(blocks, len(weights), piece, width)
    across = jnp.transpose(across, (1, 0, 2, 3)).reshape(len(weights), blocks * piece, width)
    gathered = lax.all_gather(across, CTX, axis=1, tiled=False)
    return tuple(gathered[index].reshape(-1, width) for index in range(len(weights)))


def to_gathered(values, blocks, piece):
    lead = values.shape[:-1]
    split = values.reshape(lead + (blocks, -1, piece))
    order = tuple(range(len(lead))) + (len(lead) + 1, len(lead), len(lead) + 2)
    return jnp.transpose(split, order).reshape(values.shape)


def from_gathered(values, blocks, piece):
    lead = values.shape[:-1]
    split = values.reshape(lead + (-1, blocks, piece))
    order = tuple(range(len(lead))) + (len(lead) + 1, len(lead), len(lead) + 2)
    return jnp.transpose(split, order).reshape(values.shape)


def weight_grads(pairs, factor, wait_for):
    width = pairs[0][0].shape[1]
    outer, chips, cores = lax.axis_size("dp"), lax.axis_size("cy"), lax.axis_size("core")
    mine = lax.axis_index("core")
    swap = [(0, 1), (1, 0)]
    blocks = []
    for left, right in pairs:
        other_left, other_right = lax.ppermute((left, right), "core", swap)
        both_left = jnp.concatenate([left, other_left], 0)
        both_right = jnp.concatenate([right, other_right], 0)
        tokens = both_left.shape[0]
        picked = both_left.reshape(tokens, outer * chips, cores, -1)
        picked = lax.dynamic_index_in_dim(picked, mine, 2, False).reshape(tokens, -1)
        made = lax.dot_general(
            picked, both_right, (((0,), (0,)), ((), ())), preferred_element_type=jnp.float32
        )
        blocks.append((factor * made).reshape(outer, chips, -1, width))
    rows = blocks[0].shape[2]
    stacked = jnp.concatenate(blocks, 2)
    stacked = jnp.transpose(stacked, (1, 0, 2, 3)).reshape(-1, width)
    stacked, _ = lax.optimization_barrier((stacked, wait_for))
    share = lax.all_to_all(
        stacked.reshape(chips, -1, width).astype(jnp.bfloat16), "cy", 0, 0, tiled=False
    ).astype(jnp.float32).sum(0)
    share = lax.all_to_all(
        share.reshape(outer, -1, width), "dp", 0, 0, tiled=False
    ).sum(0)
    return tuple(share[index * rows : (index + 1) * rows] for index in range(len(pairs)))


def on_device(y_first, x_second, grad_first, grad_second, w_query, w_key, w_value, w_out):
    batch, tokens_here, width = y_first.shape
    owners = lax.axis_size("dp") * lax.axis_size(CTX)
    factor = float(batch * tokens_here * owners) ** (-0.5)
    piece = w_query.shape[0] // lax.axis_size(CTX)
    blocks = lax.axis_size("dp")
    full_query, full_key, full_value, full_out = gather_rows(
        (w_query, w_key, w_value, w_out), piece
    )
    second_wide = x_second.astype(jnp.float32)
    inv_rms = lax.rsqrt(jnp.mean(second_wide * second_wide, -1, keepdims=True) + 1e-06)
    normed_wide = second_wide * inv_rms
    normed = normed_wide.astype(jnp.bfloat16)
    normed_moved = to_gathered(normed, blocks, piece)

    def project(weight):
        made = jnp.einsum("btd,df->btf", normed_moved, weight, preferred_element_type=jnp.float32)
        return made.astype(jnp.bfloat16).reshape(batch, tokens_here, HEADS, HEAD_DIM)

    queries = project(full_query)
    key_rows = project(full_key)
    values = project(full_value)
    local_state = jnp.einsum(
        "bthe,bthf->bhef", key_rows, values, preferred_element_type=jnp.float32
    )
    before = state_sum(local_state, False).astype(jnp.bfloat16)
    causal = jnp.tril(jnp.ones((tokens_here, tokens_here), dtype=bool))
    scores = jnp.einsum("bthe,bshe->bhts", queries, key_rows, preferred_element_type=jnp.float32)
    scores = jnp.where(causal[None, None], scores, 0.0).astype(jnp.bfloat16)
    mixed = jnp.einsum("bhts,bshf->bthf", scores, values, preferred_element_type=jnp.float32)
    mixed = mixed + jnp.einsum(
        "bthe,bhef->bthf", queries, before, preferred_element_type=jnp.float32
    )
    inv_head = lax.rsqrt(jnp.mean(mixed * mixed, -1, keepdims=True) + 1e-06)
    unit = mixed * inv_head
    attn_out = unit.astype(jnp.bfloat16).reshape(batch, tokens_here, width)
    attn_moved = to_gathered(attn_out, blocks, piece)
    attended = jnp.einsum("btf,fd->btd", attn_moved, full_out, preferred_element_type=jnp.float32)
    x_first = (y_first.astype(jnp.float32) - attended).astype(jnp.bfloat16)
    grad_unit = jnp.einsum("btd,fd->btf", grad_first, full_out, preferred_element_type=jnp.float32)
    grad_unit = from_gathered(grad_unit, blocks, piece)
    grad_unit = grad_unit.reshape(batch, tokens_here, HEADS, HEAD_DIM)
    grad_mixed = inv_head * (grad_unit - unit * jnp.mean(grad_unit * unit, -1, keepdims=True))
    grad_mixed = grad_mixed.astype(jnp.bfloat16)
    score_grad = jnp.einsum(
        "bthf,bshf->bhts", grad_mixed, values, preferred_element_type=jnp.float32
    )
    score_grad = jnp.where(causal[None, None], score_grad, 0.0).astype(jnp.bfloat16)
    grad_local = jnp.einsum(
        "bthe,bthf->bhef", queries, grad_mixed, preferred_element_type=jnp.float32
    )
    after_state = state_sum(grad_local, True).astype(jnp.bfloat16)
    query_grad = jnp.einsum(
        "bhts,bshe->bthe", score_grad, key_rows, preferred_element_type=jnp.float32
    )
    query_grad = query_grad + jnp.einsum(
        "bthf,bhef->bthe", grad_mixed, before, preferred_element_type=jnp.float32
    )
    key_grad = jnp.einsum(
        "bhts,bthe->bshe", score_grad, queries, preferred_element_type=jnp.float32
    )
    key_grad = key_grad + jnp.einsum(
        "bshf,bhef->bshe", values, after_state, preferred_element_type=jnp.float32
    )
    value_grad = jnp.einsum(
        "bhts,bthf->bshf", scores, grad_mixed, preferred_element_type=jnp.float32
    )
    value_grad = value_grad + jnp.einsum(
        "bshe,bhef->bshf", key_rows, after_state, preferred_element_type=jnp.float32
    )
    query_grad = query_grad.astype(jnp.bfloat16).reshape(batch, tokens_here, width)
    key_grad = key_grad.astype(jnp.bfloat16).reshape(batch, tokens_here, width)
    value_grad = value_grad.astype(jnp.bfloat16).reshape(batch, tokens_here, width)
    grad_normed = jnp.einsum(
        "btf,df->btd", query_grad, full_query, preferred_element_type=jnp.float32
    )
    grad_normed = grad_normed + jnp.einsum(
        "btf,df->btd", key_grad, full_key, preferred_element_type=jnp.float32
    )
    grad_normed = grad_normed + jnp.einsum(
        "btf,df->btd", value_grad, full_value, preferred_element_type=jnp.float32
    )
    grad_normed = from_gathered(grad_normed, blocks, piece)
    back = inv_rms * (
        grad_normed - normed_wide * jnp.mean(grad_normed * normed_wide, -1, keepdims=True)
    )
    grad_x_second = (grad_second.astype(jnp.float32) + back).astype(jnp.bfloat16)
    pairs = (
        (normed.reshape(-1, width), query_grad.reshape(-1, width)),
        (attn_out.reshape(-1, width), grad_first.reshape(-1, width)),
    )
    grad_query, grad_out = weight_grads(pairs, factor, after_state)
    return (x_first, grad_x_second, grad_query, grad_out)


def solution(mesh):
    dp, ctx = mesh.devices.shape
    fine = Mesh(mesh.devices.reshape(dp, ctx // 2, 2), ("dp", "cy", "core"))
    ctx_axes = ("cy", "core")
    rows = P("dp", ctx_axes, None)
    placed = (rows, rows, rows, rows, P("dp", None), P("dp", None), P("dp", None), P("dp", None))
    return jax.shard_map(
        on_device,
        mesh=fine,
        in_specs=placed,
        out_specs=(rows, rows, P(("dp",) + ctx_axes, None), P(("dp",) + ctx_axes, None)),
        check_vma=False,
    )
```

```python
import jax
import jax.numpy as jnp
from jax import lax
from jax.sharding import Mesh, PartitionSpec as P

HEADS = 8
HEAD_DIM = 128
CTX = ("cy", "core")


def state_sum(shard, later):
    chips = lax.axis_size("cy")
    chip = lax.axis_index("cy")
    core = lax.axis_index("core")
    swap = [(0, 1), (1, 0)]
    partner = lax.ppermute(shard, "core", swap)
    both = shard + partner
    half = shard.shape[1] // 2
    mine = lax.dynamic_slice_in_dim(both, core * half, half, 1)
    total = mine
    step = 1
    while step < chips:
        if later:
            pairs = [(source, source - step) for source in range(step, chips)]
        else:
            pairs = [(source, source + step) for source in range(chips - step)]
        total = total + lax.ppermute(total, "cy", pairs)
        step *= 2
    summed = total - mine
    other = lax.ppermute(summed, "core", swap)
    first = jnp.where(core == 0, summed, other)
    second = jnp.where(core == 0, other, summed)
    across = jnp.concatenate([first, second], 1)
    inside = (core == 0) if later else (core == 1)
    return across + jnp.where(inside, partner, 0.0)


def gather_rows(weights, piece):
    place = lax.axis_index(CTX)
    width = weights[0].shape[1]
    blocks = lax.axis_size("dp")
    parts = [lax.dynamic_slice_in_dim(weight, place * piece, piece, 0) for weight in weights]
    joined = jnp.concatenate(parts, 0)
    copies = jnp.broadcast_to(joined[None], (blocks,) + joined.shape)
    across = lax.all_to_all(copies, "dp", 0, 0, tiled=False)
    across = across.reshape(blocks, len(weights), piece, width)
    across = jnp.transpose(across, (1, 0, 2, 3)).reshape(len(weights), blocks * piece, width)
    gathered = lax.all_gather(across, CTX, axis=1, tiled=False)
    return tuple(gathered[index].reshape(-1, width) for index in range(len(weights)))


def to_gathered(values, blocks, piece):
    lead = values.shape[:-1]
    split = values.reshape(lead + (blocks, -1, piece))
    order = tuple(range(len(lead))) + (len(lead) + 1, len(lead), len(lead) + 2)
    return jnp.transpose(split, order).reshape(values.shape)


def from_gathered(values, blocks, piece):
    lead = values.shape[:-1]
    split = values.reshape(lead + (-1, blocks, piece))
    order = tuple(range(len(lead))) + (len(lead) + 1, len(lead), len(lead) + 2)
    return jnp.transpose(split, order).reshape(values.shape)


def weight_grads(pairs, factor, wait_for):
    width = pairs[0][0].shape[1]
    outer, chips, cores = lax.axis_size("dp"), lax.axis_size("cy"), lax.axis_size("core")
    mine = lax.axis_index("core")
    swap = [(0, 1), (1, 0)]
    blocks = []
    for left, right in pairs:
        other_left, other_right = lax.ppermute((left, right), "core", swap)
        both_left = jnp.concatenate([left, other_left], 0)
        both_right = jnp.concatenate([right, other_right], 0)
        tokens = both_left.shape[0]
        picked = both_left.reshape(tokens, outer * chips, cores, -1)
        picked = lax.dynamic_index_in_dim(picked, mine, 2, False).reshape(tokens, -1)
        made = lax.dot_general(
            picked, both_right, (((0,), (0,)), ((), ())), preferred_element_type=jnp.float32
        )
        blocks.append((factor * made).reshape(outer, chips, -1, width))
    rows = blocks[0].shape[2]
    stacked = jnp.concatenate(blocks, 2)
    stacked = jnp.transpose(stacked, (1, 0, 2, 3)).reshape(-1, width)
    stacked, _ = lax.optimization_barrier((stacked, wait_for))
    share = lax.all_to_all(
        stacked.reshape(chips, -1, width).astype(jnp.bfloat16), "cy", 0, 0, tiled=False
    ).astype(jnp.float32).sum(0)
    share = lax.all_to_all(
        share.reshape(outer, -1, width), "dp", 0, 0, tiled=False
    ).sum(0)
    return tuple(share[index * rows : (index + 1) * rows] for index in range(len(pairs)))


def on_device(y_first, x_second, grad_first, grad_second, w_query, w_key, w_value, w_out):
    batch, tokens_here, width = y_first.shape
    owners = lax.axis_size("dp") * lax.axis_size(CTX)
    factor = float(batch * tokens_here * owners) ** (-0.5)
    piece = w_query.shape[0] // lax.axis_size(CTX)
    blocks = lax.axis_size("dp")
    full_query, full_key, full_value, full_out = gather_rows(
        (w_query, w_key, w_value, w_out), piece
    )
    second_wide = x_second.astype(jnp.float32)
    inv_rms = lax.rsqrt(jnp.mean(second_wide * second_wide, -1, keepdims=True) + 1e-06)
    normed_wide = second_wide * inv_rms
    normed = normed_wide.astype(jnp.bfloat16)
    normed_moved = to_gathered(normed, blocks, piece)

    def project(weight):
        made = jnp.einsum("btd,df->btf", normed_moved, weight, preferred_element_type=jnp.float32)
        return made.astype(jnp.bfloat16).reshape(batch, tokens_here, HEADS, HEAD_DIM)

    queries = project(full_query)
    key_rows = project(full_key)
    values = project(full_value)
    local_state = jnp.einsum(
        "bthe,bthf->bhef", key_rows, values, preferred_element_type=jnp.float32
    )
    before = state_sum(local_state, False).astype(jnp.bfloat16)
    causal = jnp.tril(jnp.ones((tokens_here, tokens_here), dtype=bool))
    scores = jnp.einsum("bthe,bshe->bhts", queries, key_rows, preferred_element_type=jnp.float32)
    scores = jnp.where(causal[None, None], scores, 0.0).astype(jnp.bfloat16)
    mixed = jnp.einsum("bhts,bshf->bthf", scores, values, preferred_element_type=jnp.float32)
    mixed = mixed + jnp.einsum(
        "bthe,bhef->bthf", queries, before, preferred_element_type=jnp.float32
    )
    inv_head = lax.rsqrt(jnp.mean(mixed * mixed, -1, keepdims=True) + 1e-06)
    unit = mixed * inv_head
    attn_out = unit.astype(jnp.bfloat16).reshape(batch, tokens_here, width)
    attn_moved = to_gathered(attn_out, blocks, piece)
    attended = jnp.einsum("btf,fd->btd", attn_moved, full_out, preferred_element_type=jnp.float32)
    x_first = (y_first.astype(jnp.float32) - attended).astype(jnp.bfloat16)
    grad_unit = jnp.einsum("btd,fd->btf", grad_first, full_out, preferred_element_type=jnp.float32)
    grad_unit = from_gathered(grad_unit, blocks, piece)
    grad_unit = grad_unit.reshape(batch, tokens_here, HEADS, HEAD_DIM)
    grad_mixed = inv_head * (grad_unit - unit * jnp.mean(grad_unit * unit, -1, keepdims=True))
    grad_mixed = grad_mixed.astype(jnp.bfloat16)
    score_grad = jnp.einsum(
        "bthf,bshf->bhts", grad_mixed, values, preferred_element_type=jnp.float32
    )
    score_grad = jnp.where(causal[None, None], score_grad, 0.0).astype(jnp.bfloat16)
    grad_local = jnp.einsum(
        "bthe,bthf->bhef", queries, grad_mixed, preferred_element_type=jnp.float32
    )
    after_state = state_sum(grad_local, True).astype(jnp.bfloat16)
    query_grad = jnp.einsum(
        "bhts,bshe->bthe", score_grad, key_rows, preferred_element_type=jnp.float32
    )
    query_grad = query_grad + jnp.einsum(
        "bthf,bhef->bthe", grad_mixed, before, preferred_element_type=jnp.float32
    )
    key_grad = jnp.einsum(
        "bhts,bthe->bshe", score_grad, queries, preferred_element_type=jnp.float32
    )
    key_grad = key_grad + jnp.einsum(
        "bshf,bhef->bshe", values, after_state, preferred_element_type=jnp.float32
    )
    value_grad = jnp.einsum(
        "bhts,bthf->bshf", scores, grad_mixed, preferred_element_type=jnp.float32
    )
    value_grad = value_grad + jnp.einsum(
        "bshe,bhef->bshf", key_rows, after_state, preferred_element_type=jnp.float32
    )
    query_grad = query_grad.astype(jnp.bfloat16).reshape(batch, tokens_here, width)
    key_grad = key_grad.astype(jnp.bfloat16).reshape(batch, tokens_here, width)
    value_grad = value_grad.astype(jnp.bfloat16).reshape(batch, tokens_here, width)
    grad_normed = jnp.einsum(
        "btf,df->btd", query_grad, full_query, preferred_element_type=jnp.float32
    )
    grad_normed = grad_normed + jnp.einsum(
        "btf,df->btd", key_grad, full_key, preferred_element_type=jnp.float32
    )
    grad_normed = grad_normed + jnp.einsum(
        "btf,df->btd", value_grad, full_value, preferred_element_type=jnp.float32
    )
    grad_normed = from_gathered(grad_normed, blocks, piece)
    back = inv_rms * (
        grad_normed - normed_wide * jnp.mean(grad_normed * normed_wide, -1, keepdims=True)
    )
    grad_x_second = (grad_second.astype(jnp.float32) + back).astype(jnp.bfloat16)
    pairs = (
        (normed.reshape(-1, width), query_grad.reshape(-1, width)),
        (attn_out.reshape(-1, width), grad_first.reshape(-1, width)),
    )
    grad_query, grad_out = weight_grads(pairs, factor, after_state)
    return (x_first, grad_x_second, grad_query, grad_out)


def solution(mesh):
    dp, ctx = mesh.devices.shape
    fine = Mesh(mesh.devices.reshape(dp, ctx // 2, 2), ("dp", "cy", "core"))
    ctx_axes = ("cy", "core")
    rows = P("dp", ctx_axes, None)
    placed = (rows, rows, rows, rows, P("dp", None), P("dp", None), P("dp", None), P("dp", None))
    return jax.shard_map(
        on_device,
        mesh=fine,
        in_specs=placed,
        out_specs=(rows, rows, P(("dp",) + ctx_axes, None), P(("dp",) + ctx_axes, None)),
        check_vma=False,
    )
```

```python
import jax
import jax.numpy as jnp
from jax import lax
from jax.sharding import Mesh, PartitionSpec as P

HEADS = 8
HEAD_DIM = 128
CTX = ("cy", "core")


def state_sum(shard, later):
    chips = lax.axis_size("cy")
    chip = lax.axis_index("cy")
    core = lax.axis_index("core")
    swap = [(0, 1), (1, 0)]
    partner = lax.ppermute(shard, "core", swap)
    both = shard + partner
    half = shard.shape[1] // 2
    mine = lax.dynamic_slice_in_dim(both, core * half, half, 1)
    total = mine
    step = 1
    while step < chips:
        if later:
            pairs = [(source, source - step) for source in range(step, chips)]
        else:
            pairs = [(source, source + step) for source in range(chips - step)]
        total = total + lax.ppermute(total, "cy", pairs)
        step *= 2
    summed = total - mine
    other = lax.ppermute(summed, "core", swap)
    first = jnp.where(core == 0, summed, other)
    second = jnp.where(core == 0, other, summed)
    across = jnp.concatenate([first, second], 1)
    inside = (core == 0) if later else (core == 1)
    return across + jnp.where(inside, partner, 0.0)


def gather_rows(weights, piece):
    place = lax.axis_index(CTX)
    width = weights[0].shape[1]
    blocks = lax.axis_size("dp")
    parts = [lax.dynamic_slice_in_dim(weight, place * piece, piece, 0) for weight in weights]
    joined = jnp.concatenate(parts, 0)
    copies = jnp.broadcast_to(joined[None], (blocks,) + joined.shape)
    across = lax.all_to_all(copies, "dp", 0, 0, tiled=False)
    across = across.reshape(blocks, len(weights), piece, width)
    across = jnp.transpose(across, (1, 0, 2, 3)).reshape(len(weights), blocks * piece, width)
    gathered = lax.all_gather(across, CTX, axis=1, tiled=False)
    return tuple(gathered[index].reshape(-1, width) for index in range(len(weights)))


def to_gathered(values, blocks, piece):
    lead = values.shape[:-1]
    split = values.reshape(lead + (blocks, -1, piece))
    order = tuple(range(len(lead))) + (len(lead) + 1, len(lead), len(lead) + 2)
    return jnp.transpose(split, order).reshape(values.shape)


def from_gathered(values, blocks, piece):
    lead = values.shape[:-1]
    split = values.reshape(lead + (-1, blocks, piece))
    order = tuple(range(len(lead))) + (len(lead) + 1, len(lead), len(lead) + 2)
    return jnp.transpose(split, order).reshape(values.shape)


def weight_grads(pairs, factor):
    width = pairs[0][0].shape[1]
    outer, chips, cores = lax.axis_size("dp"), lax.axis_size("cy"), lax.axis_size("core")
    mine = lax.axis_index("core")
    swap = [(0, 1), (1, 0)]
    blocks = []
    for left, right in pairs:
        other_left, other_right = lax.ppermute((left, right), "core", swap)
        both_left = jnp.concatenate([left, other_left], 0)
        both_right = jnp.concatenate([right, other_right], 0)
        tokens = both_left.shape[0]
        picked = both_left.reshape(tokens, outer * chips, cores, -1)
        picked = lax.dynamic_index_in_dim(picked, mine, 2, False).reshape(tokens, -1)
        made = lax.dot_general(
            picked, both_right, (((0,), (0,)), ((), ())), preferred_element_type=jnp.float32
        )
        blocks.append((factor * made).reshape(outer, chips, -1, width))
    rows = blocks[0].shape[2]
    stacked = jnp.concatenate(blocks, 2)
    stacked = jnp.transpose(stacked, (1, 0, 2, 3)).reshape(-1, width)
    share = lax.all_to_all(
        stacked.reshape(chips, -1, width).astype(jnp.bfloat16), "cy", 0, 0, tiled=False
    ).astype(jnp.float32).sum(0)
    share = lax.all_to_all(
        share.reshape(outer, -1, width), "dp", 0, 0, tiled=False
    ).sum(0)
    return tuple(share[index * rows : (index + 1) * rows] for index in range(len(pairs)))


def on_device(y_first, x_second, grad_first, grad_second, w_query, w_key, w_value, w_out):
    batch, tokens_here, width = y_first.shape
    owners = lax.axis_size("dp") * lax.axis_size(CTX)
    factor = float(batch * tokens_here * owners) ** (-0.5)
    piece = w_query.shape[0] // lax.axis_size(CTX)
    blocks = lax.axis_size("dp")
    full_query, full_key, full_value, full_out = gather_rows(
        (w_query, w_key, w_value, w_out), piece
    )
    second_wide = x_second.astype(jnp.float32)
    inv_rms = lax.rsqrt(jnp.mean(second_wide * second_wide, -1, keepdims=True) + 1e-06)
    normed_wide = second_wide * inv_rms
    normed = normed_wide.astype(jnp.bfloat16)
    normed_moved = to_gathered(normed, blocks, piece)

    def project(weight):
        made = jnp.einsum("btd,df->btf", normed_moved, weight, preferred_element_type=jnp.float32)
        return made.astype(jnp.bfloat16).reshape(batch, tokens_here, HEADS, HEAD_DIM)

    queries = project(full_query)
    key_rows = project(full_key)
    values = project(full_value)
    local_state = jnp.einsum(
        "bthe,bthf->bhef", key_rows, values, preferred_element_type=jnp.float32
    )
    before = state_sum(local_state, False).astype(jnp.bfloat16)
    causal = jnp.tril(jnp.ones((tokens_here, tokens_here), dtype=bool))
    scores = jnp.einsum("bthe,bshe->bhts", queries, key_rows, preferred_element_type=jnp.float32)
    scores = jnp.where(causal[None, None], scores, 0.0).astype(jnp.bfloat16)
    mixed = jnp.einsum("bhts,bshf->bthf", scores, values, preferred_element_type=jnp.float32)
    mixed = mixed + jnp.einsum(
        "bthe,bhef->bthf", queries, before, preferred_element_type=jnp.float32
    )
    inv_head = lax.rsqrt(jnp.mean(mixed * mixed, -1, keepdims=True) + 1e-06)
    unit = mixed * inv_head
    attn_out = unit.astype(jnp.bfloat16).reshape(batch, tokens_here, width)
    attn_moved = to_gathered(attn_out, blocks, piece)
    attended = jnp.einsum("btf,fd->btd", attn_moved, full_out, preferred_element_type=jnp.float32)
    x_first = (y_first.astype(jnp.float32) - attended).astype(jnp.bfloat16)
    grad_unit = jnp.einsum("btd,fd->btf", grad_first, full_out, preferred_element_type=jnp.float32)
    grad_unit = from_gathered(grad_unit, blocks, piece)
    grad_unit = grad_unit.reshape(batch, tokens_here, HEADS, HEAD_DIM)
    grad_mixed = inv_head * (grad_unit - unit * jnp.mean(grad_unit * unit, -1, keepdims=True))
    grad_mixed = grad_mixed.astype(jnp.bfloat16)
    score_grad = jnp.einsum(
        "bthf,bshf->bhts", grad_mixed, values, preferred_element_type=jnp.float32
    )
    score_grad = jnp.where(causal[None, None], score_grad, 0.0).astype(jnp.bfloat16)
    grad_local = jnp.einsum(
        "bthe,bthf->bhef", queries, grad_mixed, preferred_element_type=jnp.float32
    )
    after_state = state_sum(grad_local, True).astype(jnp.bfloat16)
    query_grad = jnp.einsum(
        "bhts,bshe->bthe", score_grad, key_rows, preferred_element_type=jnp.float32
    )
    query_grad = query_grad + jnp.einsum(
        "bthf,bhef->bthe", grad_mixed, before, preferred_element_type=jnp.float32
    )
    key_grad = jnp.einsum(
        "bhts,bthe->bshe", score_grad, queries, preferred_element_type=jnp.float32
    )
    key_grad = key_grad + jnp.einsum(
        "bshf,bhef->bshe", values, after_state, preferred_element_type=jnp.float32
    )
    value_grad = jnp.einsum(
        "bhts,bthf->bshf", scores, grad_mixed, preferred_element_type=jnp.float32
    )
    value_grad = value_grad + jnp.einsum(
        "bshe,bhef->bshf", key_rows, after_state, preferred_element_type=jnp.float32
    )
    query_grad = query_grad.astype(jnp.bfloat16).reshape(batch, tokens_here, width)
    key_grad = key_grad.astype(jnp.bfloat16).reshape(batch, tokens_here, width)
    value_grad = value_grad.astype(jnp.bfloat16).reshape(batch, tokens_here, width)
    grad_normed = jnp.einsum(
        "btf,df->btd", query_grad, full_query, preferred_element_type=jnp.float32
    )
    grad_normed = grad_normed + jnp.einsum(
        "btf,df->btd", key_grad, full_key, preferred_element_type=jnp.float32
    )
    grad_normed = grad_normed + jnp.einsum(
        "btf,df->btd", value_grad, full_value, preferred_element_type=jnp.float32
    )
    grad_normed = from_gathered(grad_normed, blocks, piece)
    back = inv_rms * (
        grad_normed - normed_wide * jnp.mean(grad_normed * normed_wide, -1, keepdims=True)
    )
    grad_x_second = (grad_second.astype(jnp.float32) + back).astype(jnp.bfloat16)
    pairs = (
        (normed.reshape(-1, width), query_grad.reshape(-1, width)),
        (attn_out.reshape(-1, width), grad_first.reshape(-1, width)),
    )
    grad_query, grad_out = weight_grads(pairs, factor)
    return (x_first, grad_x_second, grad_query, grad_out)


def solution(mesh):
    dp, ctx = mesh.devices.shape
    fine = Mesh(mesh.devices.reshape(dp, ctx // 2, 2), ("dp", "cy", "core"))
    ctx_axes = ("cy", "core")
    rows = P("dp", ctx_axes, None)
    placed = (rows, rows, rows, rows, P("dp", None), P("dp", None), P("dp", None), P("dp", None))
    return jax.shard_map(
        on_device,
        mesh=fine,
        in_specs=placed,
        out_specs=(rows, rows, P(("dp",) + ctx_axes, None), P(("dp",) + ctx_axes, None)),
        check_vma=False,
    )
```

```python
import jax
import jax.numpy as jnp
from jax import lax
from jax.sharding import Mesh, PartitionSpec as P

HEADS = 8
HEAD_DIM = 128
CTX = ("cy", "core")


def state_sum(shard, later):
    chips = lax.axis_size("cy")
    chip = lax.axis_index("cy")
    core = lax.axis_index("core")
    swap = [(0, 1), (1, 0)]
    partner = lax.ppermute(shard, "core", swap)
    both = shard + partner
    half = shard.shape[1] // 2
    mine = lax.dynamic_slice_in_dim(both, core * half, half, 1)
    total = mine
    step = 1
    while step < chips:
        if later:
            pairs = [(source, source - step) for source in range(step, chips)]
        else:
            pairs = [(source, source + step) for source in range(chips - step)]
        total = total + lax.ppermute(total, "cy", pairs)
        step *= 2
    summed = total - mine
    other = lax.ppermute(summed, "core", swap)
    first = jnp.where(core == 0, summed, other)
    second = jnp.where(core == 0, other, summed)
    across = jnp.concatenate([first, second], 1)
    inside = (core == 0) if later else (core == 1)
    return across + jnp.where(inside, partner, 0.0)


def gather_rows(weights, piece):
    place = lax.axis_index(CTX)
    width = weights[0].shape[1]
    blocks = lax.axis_size("dp")
    parts = [lax.dynamic_slice_in_dim(weight, place * piece, piece, 0) for weight in weights]
    joined = jnp.concatenate(parts, 0)
    copies = jnp.broadcast_to(joined[None], (blocks,) + joined.shape)
    across = lax.all_to_all(copies, "dp", 0, 0, tiled=False)
    across = across.reshape(blocks, len(weights), piece, width)
    across = jnp.transpose(across, (1, 0, 2, 3)).reshape(len(weights), blocks * piece, width)
    gathered = lax.all_gather(across, CTX, axis=1, tiled=False)
    return tuple(gathered[index].reshape(-1, width) for index in range(len(weights)))


def to_gathered(values, blocks, piece):
    lead = values.shape[:-1]
    split = values.reshape(lead + (blocks, -1, piece))
    order = tuple(range(len(lead))) + (len(lead) + 1, len(lead), len(lead) + 2)
    return jnp.transpose(split, order).reshape(values.shape)


def from_gathered(values, blocks, piece):
    lead = values.shape[:-1]
    split = values.reshape(lead + (-1, blocks, piece))
    order = tuple(range(len(lead))) + (len(lead) + 1, len(lead), len(lead) + 2)
    return jnp.transpose(split, order).reshape(values.shape)


def weight_grads(pairs, factor, wait_for):
    width = pairs[0][0].shape[1]
    outer, chips, cores = lax.axis_size("dp"), lax.axis_size("cy"), lax.axis_size("core")
    mine = lax.axis_index("core")
    swap = [(0, 1), (1, 0)]
    blocks = []
    for left, right in pairs:
        other_left, other_right = lax.ppermute((left, right), "core", swap)
        both_left = jnp.concatenate([left, other_left], 0)
        both_right = jnp.concatenate([right, other_right], 0)
        tokens = both_left.shape[0]
        picked = both_left.reshape(tokens, outer * chips, cores, -1)
        picked = lax.dynamic_index_in_dim(picked, mine, 2, False).reshape(tokens, -1)
        made = lax.dot_general(
            picked, both_right, (((0,), (0,)), ((), ())), preferred_element_type=jnp.float32
        )
        blocks.append((factor * made).reshape(outer, chips, -1, width))
    rows = blocks[0].shape[2]
    stacked = jnp.concatenate(blocks, 2).reshape(outer * chips, -1, width)
    stacked, _ = lax.optimization_barrier((stacked, wait_for))
    share = lax.all_to_all(
        stacked.astype(jnp.bfloat16), ("dp", "cy"), 0, 0, tiled=False
    ).astype(jnp.float32).sum(0)
    return tuple(share[index * rows : (index + 1) * rows] for index in range(len(pairs)))


def on_device(y_first, x_second, grad_first, grad_second, w_query, w_key, w_value, w_out):
    batch, tokens_here, width = y_first.shape
    owners = lax.axis_size("dp") * lax.axis_size(CTX)
    factor = float(batch * tokens_here * owners) ** (-0.5)
    piece = w_query.shape[0] // lax.axis_size(CTX)
    blocks = lax.axis_size("dp")
    full_query, full_key, full_value, full_out = gather_rows(
        (w_query, w_key, w_value, w_out), piece
    )
    second_wide = x_second.astype(jnp.float32)
    inv_rms = lax.rsqrt(jnp.mean(second_wide * second_wide, -1, keepdims=True) + 1e-06)
    normed_wide = second_wide * inv_rms
    normed = normed_wide.astype(jnp.bfloat16)
    normed_moved = to_gathered(normed, blocks, piece)

    def project(weight):
        made = jnp.einsum("btd,df->btf", normed_moved, weight, preferred_element_type=jnp.float32)
        return made.astype(jnp.bfloat16).reshape(batch, tokens_here, HEADS, HEAD_DIM)

    queries = project(full_query)
    key_rows = project(full_key)
    values = project(full_value)
    local_state = jnp.einsum(
        "bthe,bthf->bhef", key_rows, values, preferred_element_type=jnp.float32
    )
    before = state_sum(local_state, False).astype(jnp.bfloat16)
    causal = jnp.tril(jnp.ones((tokens_here, tokens_here), dtype=bool))
    scores = jnp.einsum("bthe,bshe->bhts", queries, key_rows, preferred_element_type=jnp.float32)
    scores = jnp.where(causal[None, None], scores, 0.0).astype(jnp.bfloat16)
    mixed = jnp.einsum("bhts,bshf->bthf", scores, values, preferred_element_type=jnp.float32)
    mixed = mixed + jnp.einsum(
        "bthe,bhef->bthf", queries, before, preferred_element_type=jnp.float32
    )
    inv_head = lax.rsqrt(jnp.mean(mixed * mixed, -1, keepdims=True) + 1e-06)
    unit = mixed * inv_head
    attn_out = unit.astype(jnp.bfloat16).reshape(batch, tokens_here, width)
    attn_moved = to_gathered(attn_out, blocks, piece)
    attended = jnp.einsum("btf,fd->btd", attn_moved, full_out, preferred_element_type=jnp.float32)
    x_first = (y_first.astype(jnp.float32) - attended).astype(jnp.bfloat16)
    grad_unit = jnp.einsum("btd,fd->btf", grad_first, full_out, preferred_element_type=jnp.float32)
    grad_unit = from_gathered(grad_unit, blocks, piece)
    grad_unit = grad_unit.reshape(batch, tokens_here, HEADS, HEAD_DIM)
    grad_mixed = inv_head * (grad_unit - unit * jnp.mean(grad_unit * unit, -1, keepdims=True))
    grad_mixed = grad_mixed.astype(jnp.bfloat16)
    score_grad = jnp.einsum(
        "bthf,bshf->bhts", grad_mixed, values, preferred_element_type=jnp.float32
    )
    score_grad = jnp.where(causal[None, None], score_grad, 0.0).astype(jnp.bfloat16)
    grad_local = jnp.einsum(
        "bthe,bthf->bhef", queries, grad_mixed, preferred_element_type=jnp.float32
    )
    after_state = state_sum(grad_local, True).astype(jnp.bfloat16)
    query_grad = jnp.einsum(
        "bhts,bshe->bthe", score_grad, key_rows, preferred_element_type=jnp.float32
    )
    query_grad = query_grad + jnp.einsum(
        "bthf,bhef->bthe", grad_mixed, before, preferred_element_type=jnp.float32
    )
    key_grad = jnp.einsum(
        "bhts,bthe->bshe", score_grad, queries, preferred_element_type=jnp.float32
    )
    key_grad = key_grad + jnp.einsum(
        "bshf,bhef->bshe", values, after_state, preferred_element_type=jnp.float32
    )
    value_grad = jnp.einsum(
        "bhts,bthf->bshf", scores, grad_mixed, preferred_element_type=jnp.float32
    )
    value_grad = value_grad + jnp.einsum(
        "bshe,bhef->bshf", key_rows, after_state, preferred_element_type=jnp.float32
    )
    query_grad = query_grad.astype(jnp.bfloat16).reshape(batch, tokens_here, width)
    key_grad = key_grad.astype(jnp.bfloat16).reshape(batch, tokens_here, width)
    value_grad = value_grad.astype(jnp.bfloat16).reshape(batch, tokens_here, width)
    grad_normed = jnp.einsum(
        "btf,df->btd", query_grad, full_query, preferred_element_type=jnp.float32
    )
    grad_normed = grad_normed + jnp.einsum(
        "btf,df->btd", key_grad, full_key, preferred_element_type=jnp.float32
    )
    grad_normed = grad_normed + jnp.einsum(
        "btf,df->btd", value_grad, full_value, preferred_element_type=jnp.float32
    )
    grad_normed = from_gathered(grad_normed, blocks, piece)
    back = inv_rms * (
        grad_normed - normed_wide * jnp.mean(grad_normed * normed_wide, -1, keepdims=True)
    )
    grad_x_second = (grad_second.astype(jnp.float32) + back).astype(jnp.bfloat16)
    pairs = (
        (normed.reshape(-1, width), query_grad.reshape(-1, width)),
        (attn_out.reshape(-1, width), grad_first.reshape(-1, width)),
    )
    grad_query, grad_out = weight_grads(pairs, factor, after_state)
    return (x_first, grad_x_second, grad_query, grad_out)


def solution(mesh):
    dp, ctx = mesh.devices.shape
    fine = Mesh(mesh.devices.reshape(dp, ctx // 2, 2), ("dp", "cy", "core"))
    ctx_axes = ("cy", "core")
    rows = P("dp", ctx_axes, None)
    placed = (rows, rows, rows, rows, P("dp", None), P("dp", None), P("dp", None), P("dp", None))
    return jax.shard_map(
        on_device,
        mesh=fine,
        in_specs=placed,
        out_specs=(rows, rows, P(("dp",) + ctx_axes, None), P(("dp",) + ctx_axes, None)),
        check_vma=False,
    )
```
